128 devices in a mesh: seq: 16 (over x, z_hi, core), tp: 8 (over z_lo, y).
Axes of the slice: x: 4, y: 4, z: 4 (z_hi: 2, z_lo: 2; z = z_hi * 2 + z_lo), core: 2. Of those that a mesh axis runs over, the one named last changes fastest.
Arguments:
- tokens: bfloat16 [4096, 5120], P('seq', 'tp'), may hold values from -6 to 6
- norm_gain: float32 [5120], replicated, may hold values from 0.1 to 1.9
- q_weight: bfloat16 [5120, 5120], P(None, 'tp'), may hold values from -0.078125 to 0.078125
- kv_weight: bfloat16 [5120, 2, 1024], P(None, None, 'tp'), may hold values from -0.078125 to 0.078125
- out_weight: bfloat16 [5120, 5120], P('tp'), may hold values from -0.5 to 0.5
- ctx_cache: bfloat16 [16384, 2, 1024], P('seq', None, 'tp'), may hold values from -1000 to 1000, as said below
- span_start: int32 [1], replicated, may hold values from 4096 to 16384
- finished_cache: bfloat16 [4, 16384, 2, 1024], P(None, 'seq', None, 'tp'), may hold values from -6 to 6
- block_dest: int32 [1024, 1], P('seq'), may hold values from 0 to 15; in each aligned block of 64 rows (0 to 63, 64 to 127, ...) at most 8 rows name the same one
Outputs:
- attended: bfloat16 [4096, 5120], P('seq', 'tp')
- page_pool: bfloat16 [4, 32768, 2, 1024], P(None, 'seq', None, 'tp')
The draws below stay inside these ranges and needn't reach their ends.
Inputs may be any that keep to these rules, and one draw needn't show every extreme that they name: `block_dest`: among the 64 blocks of one index of seq, no decode index is named more than 8 times, and some decode index is named exactly 8 times. `ctx_cache`: keys are stored already rotated at their positions; keys may reach some hundreds in magnitude, values lie within -6 to 6.
All inputs are finite; a program needn't handle non-finite values.
Results may differ from the reference program's by a relative error of at most 0.03.
The reference program's roundings to bfloat16 on the way (of `normed`, `queries`, `rounded` and `mixed_heads`) count: a program that leaves them out, or rounds other values in their place, can miss the bound.
Values may be sent and summed in bfloat16 or wider, within the bound.
No kernel may reach another device: no remote copies, remote signals or barrier semaphores. Data moves between devices by JAX's collectives and lax.ppermute only.
A program may use at most 128 MiB of HBM per device.

```python
import math
import jax
import jax.numpy as jnp
import numpy as np
from jax import lax

D = 5120
HQ = 40
KVH = 8
HD = 128
TOK_DEV = 256
LAYERS = 4
BLK = 16
TOKENS = 4096
CTX = 16384
FIN = 16384
BLK_DEV = 64
NBLK = 1024
CAP = 8
POOL = 32768
N_SEQ = 16


def draw_ctx_cache(key, part):
    drawn = jnp.clip(jax.random.normal(key, (CTX, 2, KVH * HD), jnp.float32), -6.0, 6.0)
    return drawn.astype(jnp.bfloat16)


def levels(rng, dims, pieces, smallest, top_value):
    factor_of = 1.0
    for dim, blocks in pieces:
        steps = jax.random.uniform(jax.random.fold_in(jax.random.fold_in(rng, 6), dim), (blocks,), jnp.float32, smallest / len(pieces), top_value / len(pieces))
        factor_of = factor_of * jnp.repeat(jnp.exp(steps), dims[dim] // blocks).reshape((-1,) + (1,) * (len(dims) - 1 - dim))
    return factor_of


def deal_out(rng, own, number, rows, amount, top, reach, slope):
    ranking = jax.random.permutation(rng, amount)
    packed, common = portions_of(amount, rows * top, reach, slope, True), portions_of(amount, rows * top, reach, slope, False)
    places = jnp.arange(amount)

    def named(sizes, offset_by):
        used = int((sizes > 0).sum())
        fixed = max(1, used // 4)
        shifted = fixed + (places - fixed + offset_by * (used - fixed)) % max(1, amount - fixed)
        return jnp.zeros((amount,), jnp.int32).at[ranking[jnp.where(places < fixed, places, shifted)]].set(jnp.asarray(sizes, jnp.int32))

    sizes = jnp.where(number % 4 == 0, named(packed, number // 4), named(common, number - number // 4 - 1))
    mixed = jax.random.permutation(jax.random.fold_in(own, 3), amount)
    giver, receiver = mixed[0:amount // 2 * 2:2], mixed[1:amount // 2 * 2:2]
    room = jnp.minimum(sizes[giver] - 1, reach - sizes[receiver]) // 2
    room = jnp.where((giver == ranking[0]) | (receiver == ranking[0]) | (sizes[receiver] == 0), 0, jnp.maximum(room, 0))
    shifted = jax.random.randint(jax.random.fold_in(own, 4), (amount // 2,), 0, 1 << 20) % (room + 1)
    sizes = sizes.at[giver].add(-shifted).at[receiver].add(shifted)
    labels = jnp.searchsorted(jnp.cumsum(sizes), jnp.arange(rows * top), side="right").astype(jnp.int32)
    table = labels.reshape(top, rows).T
    table = table[jax.random.permutation(jax.random.fold_in(own, 1), rows)]
    offset_by = jax.random.randint(jax.random.fold_in(own, 2), (rows, 1), 0, top)
    return jnp.take_along_axis(table, (jnp.arange(top)[None, :] + offset_by) % top, axis=1)


def portions_of(amount, total, bound, slope, full):
    loads = [(1 << 20) // math.isqrt(standing ** slope) + 1 for standing in range(1, amount + 1)]
    largest = bound if full else min(bound, max(-(-total // amount), total * loads[0] // sum(loads)))
    least = 1 if total - largest >= amount - 1 else 0
    counts, spare = [largest] + [least] * (amount - 1), total - largest - least * (amount - 1)
    while spare > 0:
        movable = [i for i in range(1, amount) if counts[i] < largest] or [i for i in range(1, amount) if counts[i] < bound]
        pool, left = sum([loads[i] for i in movable]), spare
        for i in movable:
            addition = min(bound - counts[i], max(1, left * loads[i] // pool), spare)
            counts[i] = counts[i] + addition
            spare = spare - addition
    return np.array(counts)


def normal_values(key, shape, deviation, limit, pieces=(), held_as=jnp.bfloat16):
    entries = jax.random.normal(key, shape, jnp.float32) * deviation
    if len(pieces) > 0:
        entries = levels(key, shape, pieces, -0.22, 0.18) * entries
    return jnp.clip(entries, min=-limit, max=limit).astype(held_as)


def setup_inputs(seed: int = 0) -> dict:
    key_of = jax.random.split(jax.random.key(seed), 10)
    tokens = normal_values(key_of[0], (TOKENS, D), 1.0, 6.0, ((0, 16), (1, 8)))
    norm_gain = jnp.clip(1.0 + 0.18 * jax.random.normal(key_of[1], (D,), jnp.float32), 0.1, 1.9)
    q_weight = normal_values(key_of[2], (D, HQ * HD), D ** -0.5, 0.078125, ((1, 8),))
    kv_weight = normal_values(key_of[3], (D, 2, KVH * HD), D ** -0.5, 0.078125, ((2, 8),))
    out_weight = normal_values(key_of[4], (HQ * HD, D), HD ** -0.5, 0.5, ((0, 8),))
    ctx_cache = draw_ctx_cache(jax.random.fold_in(key_of[9], 71), 0)
    span_start = jax.random.randint(key_of[6], (1,), CTX // 4, CTX + 1).astype(jnp.int32)
    finished_cache = normal_values(key_of[7], (LAYERS, FIN, 2, KVH * HD), 1.0, 6.0, ((1, 16), (3, 8)))
    block_dest_keys = jax.random.split(jax.random.fold_in(key_of[8], 1), NBLK // BLK_DEV)
    block_dest_turns = jax.random.permutation(jax.random.fold_in(key_of[8], 3), NBLK // BLK_DEV)
    block_dest = jax.vmap(lambda own, number: deal_out(jax.random.fold_in(key_of[8], 2), own, number, BLK_DEV, N_SEQ, 1, CAP, 2))(block_dest_keys, block_dest_turns).reshape((NBLK, 1))
    return dict(tokens=tokens, norm_gain=norm_gain, q_weight=q_weight, kv_weight=kv_weight, out_weight=out_weight, ctx_cache=ctx_cache, span_start=span_start, finished_cache=finished_cache, block_dest=block_dest)


rms_eps = 1e-06
rope_base = 1000000.0
neg_fill = -1e+30

def rotate_pairs(values, positions):
    half_width = values.shape[-1] // 2
    frequency = jnp.exp(jnp.arange(half_width, dtype=jnp.float32) * (-2.0 * math.log(rope_base) / values.shape[-1]))
    angles = positions[:, None] * frequency[None, :]
    cosine = jnp.cos(angles)[:, None, :]
    sine_part = jnp.sin(angles)[:, None, :]
    first_half = values[..., :half_width]
    second_half = values[..., half_width:]
    return jnp.concatenate([first_half * cosine - second_half * sine_part, second_half * cosine + first_half * sine_part], -1)

def reference(tokens, norm_gain, q_weight, kv_weight, out_weight, ctx_cache, span_start, finished_cache, block_dest):
    head_group = HQ // KVH
    widened = tokens.astype(jnp.float32)
    normed = (widened * lax.rsqrt(lax.optimization_barrier(jnp.mean(widened * widened, axis=-1, keepdims=True)) + rms_eps) * norm_gain).astype(jnp.bfloat16)
    span_first = span_start[0]
    positions = (span_first + jnp.arange(TOKENS, dtype=jnp.int32)).astype(jnp.float32)
    queries = jnp.dot(normed, q_weight, preferred_element_type=jnp.float32).reshape(TOKENS, HQ, HD)
    queries = rotate_pairs(queries, positions).astype(jnp.bfloat16).reshape(TOKENS, KVH, head_group, HD)
    queries = lax.optimization_barrier(queries)
    projected = jnp.dot(normed, kv_weight.reshape(D, 2 * KVH * HD), preferred_element_type=jnp.float32).reshape(TOKENS, 2, KVH, HD)
    new_keys = rotate_pairs(projected[:, 0], positions).astype(jnp.bfloat16)
    new_values = projected[:, 1].astype(jnp.bfloat16)
    all_keys = jnp.concatenate([ctx_cache[:, 0].reshape(CTX, KVH, HD), new_keys], 0)
    all_values = jnp.concatenate([ctx_cache[:, 1].reshape(CTX, KVH, HD), new_values], 0)
    all_keys, all_values = lax.optimization_barrier((all_keys, all_values))
    cached_visible = jnp.arange(CTX, dtype=jnp.int32) < span_first
    span_order = jnp.arange(TOKENS, dtype=jnp.int32)

    def query_block(block_index):
        block_queries = lax.dynamic_slice_in_dim(queries, block_index * TOK_DEV, TOK_DEV, 0)
        query_order = block_index * TOK_DEV + jnp.arange(TOK_DEV, dtype=jnp.int32)
        visible = jnp.concatenate([jnp.broadcast_to(cached_visible[None, :], (TOK_DEV, CTX)), span_order[None, :] <= query_order[:, None]], 1)

        def one_head(head_index):
            head_queries = lax.dynamic_index_in_dim(block_queries, head_index, 1, keepdims=False).astype(jnp.float32)
            head_keys = lax.dynamic_index_in_dim(all_keys, head_index, 1, keepdims=False).astype(jnp.float32)
            head_values = lax.dynamic_index_in_dim(all_values, head_index, 1, keepdims=False).astype(jnp.float32)
            scores = jnp.einsum('tgd,sd->tgs', head_queries, head_keys) * HD ** (-0.5)
            visible_mask = visible[:, None, :]
            row_max = lax.optimization_barrier(jnp.max(jnp.where(visible_mask, scores, neg_fill), -1, keepdims=True))
            weights = jnp.where(visible_mask, jnp.exp(scores - row_max), 0.0)
            row_total = lax.optimization_barrier(jnp.sum(weights, -1))
            rounded = lax.optimization_barrier(weights.astype(jnp.bfloat16)).astype(jnp.float32)
            summed = jnp.einsum('tgs,sd->tgd', rounded, head_values)
            return (summed / row_total[..., None]).astype(jnp.bfloat16)
        per_head = lax.map(one_head, jnp.arange(KVH, dtype=jnp.int32))
        return jnp.transpose(per_head, (1, 0, 2, 3)).reshape(TOK_DEV, HQ * HD)
    mixed_heads = lax.map(query_block, jnp.arange(N_SEQ, dtype=jnp.int32)).reshape(TOKENS, HQ * HD)
    attended = jnp.dot(mixed_heads, out_weight, preferred_element_type=jnp.float32).astype(jnp.bfloat16)
    destination = block_dest[:, 0].reshape(N_SEQ, BLK_DEV)
    onehot = (destination[:, :, None] == jnp.arange(N_SEQ, dtype=jnp.int32)[None, None, :]).astype(jnp.int32)
    earlier_count = lax.optimization_barrier(jnp.sum((jnp.cumsum(onehot, axis=1, dtype=jnp.int32) - onehot) * onehot, axis=-1))
    source_index = jnp.arange(N_SEQ, dtype=jnp.int32)[:, None]
    target = (destination * (N_SEQ * CAP) + source_index * CAP + earlier_count).reshape(NBLK)
    blocks = finished_cache.reshape(LAYERS, NBLK, BLK, 2, KVH * HD)
    page_pool = jnp.zeros((LAYERS, N_SEQ * N_SEQ * CAP, BLK, 2, KVH * HD), finished_cache.dtype).at[:, target].set(blocks)
    page_pool = page_pool.reshape(LAYERS, POOL, 2, KVH * HD)
    return (attended, page_pool)
```

```python
import math
import functools

import jax
import jax.numpy as jnp
from jax import lax
from jax.experimental import pallas as pl
from jax.experimental.pallas import tpu as pltpu
from jax.sharding import PartitionSpec as P

D = 5120
HD = 128
LAYERS = 4
BLK = 16
CTX_BLOCK = 1024


rms_eps = 1e-06
rope_base = 1000000.0
neg_fill = -1e30


def rotate_pairs(values, positions):
    half_width = values.shape[-1] // 2
    frequency = jnp.exp(
        jnp.arange(half_width, dtype=jnp.float32) * (-2.0 * math.log(rope_base) / values.shape[-1])
    )
    angles = positions[:, None] * frequency[None, :]
    cosine = jnp.cos(angles)[:, None, :]
    sine_part = jnp.sin(angles)[:, None, :]
    first_half = values[..., :half_width]
    second_half = values[..., half_width:]
    return jnp.concatenate(
        [
            first_half * cosine - second_half * sine_part,
            second_half * cosine + first_half * sine_part,
        ],
        -1,
    )


def flash_kernel(
    scalars, q_ref, kv_ref, m_in, l_in, acc_in, m_ref, l_ref, acc_ref,
    *, block_rows, tok_rows, causal
):
    step = pl.program_id(0)
    span_first = scalars[0]
    seq_place = scalars[1]

    @pl.when(step == 0)
    def _():
        m_ref[...] = m_in[...]
        l_ref[...] = l_in[...]
        acc_ref[...] = acc_in[...]

    if causal:
        live = step <= seq_place
    else:
        live = step * block_rows < span_first

    @pl.when(live)
    def _():
        q = q_ref[...]
        k = kv_ref[:, :HD]
        v = kv_ref[:, HD:]
        scores = lax.dot_general(
            q, k, (((1,), (1,)), ((), ())), preferred_element_type=jnp.float32
        ) * HD ** (-0.5)
        col = lax.broadcasted_iota(jnp.int32, scores.shape, 1) + step * block_rows
        if causal:
            row = (lax.broadcasted_iota(jnp.int32, scores.shape, 0) & (tok_rows - 1)) + seq_place * tok_rows
            visible = col <= row
        else:
            visible = col < span_first
        row_max = m_ref[...]
        new_max = jnp.maximum(row_max, jnp.max(jnp.where(visible, scores, neg_fill), 1, keepdims=True))
        weights = jnp.where(visible, jnp.exp(scores - new_max), 0.0)
        rescale = jnp.exp(row_max - new_max)
        l_ref[...] = l_ref[...] * rescale + jnp.sum(weights, 1, keepdims=True)
        acc_ref[...] = acc_ref[...] * rescale + jnp.dot(
            weights.astype(jnp.bfloat16), v, preferred_element_type=jnp.float32
        )
        m_ref[...] = new_max


def flash_pass(scalars, queries, kv_rows, state, block_rows, tok_rows, causal):
    rows = queries.shape[0]
    block_count = kv_rows.shape[0] // block_rows
    if causal:
        def kv_map(j, s):
            return (jnp.minimum(j, s[1]), 0)
    else:
        def kv_map(j, s):
            last = (s[0] + block_rows - 1) // block_rows - 1
            return (jnp.maximum(jnp.minimum(j, last), 0), 0)
    full = lambda j, s: (0, 0)
    kernel = functools.partial(
        flash_kernel, block_rows=block_rows, tok_rows=tok_rows, causal=causal
    )
    return pl.pallas_call(
        kernel,
        out_shape=(
            jax.ShapeDtypeStruct((rows, 1), jnp.float32),
            jax.ShapeDtypeStruct((rows, 1), jnp.float32),
            jax.ShapeDtypeStruct((rows, HD), jnp.float32),
        ),
        grid_spec=pltpu.PrefetchScalarGridSpec(
            num_scalar_prefetch=1,
            grid=(block_count,),
            in_specs=[
                pl.BlockSpec((rows, HD), full),
                pl.BlockSpec((block_rows, 2 * HD), kv_map),
                pl.BlockSpec((rows, 1), full),
                pl.BlockSpec((rows, 1), full),
                pl.BlockSpec((rows, HD), full),
            ],
            out_specs=[
                pl.BlockSpec((rows, 1), full),
                pl.BlockSpec((rows, 1), full),
                pl.BlockSpec((rows, HD), full),
            ],
        ),
        compiler_params=pltpu.CompilerParams(
            dimension_semantics=("arbitrary",), vmem_limit_bytes=48 * 1024 * 1024
        ),
    )(scalars, queries, kv_rows, *state)


def on_device(
    tokens,
    norm_gain,
    q_weight,
    kv_weight,
    out_weight,
    ctx_cache,
    span_start,
    finished_cache,
    block_dest,
):
    seq_count = lax.axis_size("seq")
    seq_place = lax.axis_index("seq")
    tok_rows = tokens.shape[0]
    kv_heads = kv_weight.shape[2] // HD
    head_group = q_weight.shape[1] // HD // kv_heads
    kv_width = kv_heads * HD
    ctx_rows = ctx_cache.reshape(ctx_cache.shape[0], 2 * kv_width)
    ctx_all = lax.all_gather(ctx_rows, "seq", axis=0, tiled=True)
    gathered = lax.all_gather(tokens, "tp", axis=1, tiled=True)
    widened = gathered.astype(jnp.float32)
    normed = (
        widened
        * lax.rsqrt(jnp.mean(widened * widened, axis=-1, keepdims=True) + rms_eps)
        * norm_gain
    ).astype(jnp.bfloat16)
    span_first = span_start[0]
    positions = (span_first + seq_place * tok_rows + jnp.arange(tok_rows, dtype=jnp.int32)).astype(
        jnp.float32
    )
    queries = jnp.dot(normed, q_weight, preferred_element_type=jnp.float32).reshape(
        tok_rows, kv_heads * head_group, HD
    )
    queries = rotate_pairs(queries, positions).astype(jnp.bfloat16)
    queries = jnp.transpose(queries, (1, 0, 2)).reshape(head_group * tok_rows, HD)
    projected = jnp.dot(
        normed, kv_weight.reshape(D, 2 * kv_width), preferred_element_type=jnp.float32
    ).reshape(tok_rows, 2, kv_heads, HD)
    new_keys = (
        rotate_pairs(projected[:, 0], positions).astype(jnp.bfloat16).reshape(tok_rows, kv_width)
    )
    new_values = projected[:, 1].astype(jnp.bfloat16).reshape(tok_rows, kv_width)
    new_rows = jnp.concatenate([new_keys, new_values], 1)
    new_all = lax.all_gather(new_rows, "seq", axis=0, tiled=True)
    query_rows = head_group * tok_rows
    scalars = jnp.stack([span_first, seq_place]).astype(jnp.int32)
    empty_state = (
        jnp.full((query_rows, 1), neg_fill, jnp.float32),
        jnp.zeros((query_rows, 1), jnp.float32),
        jnp.zeros((query_rows, HD), jnp.float32),
    )
    state = flash_pass(scalars, queries, ctx_all, empty_state, CTX_BLOCK, tok_rows, False)
    row_max, row_total, summed = flash_pass(scalars, queries, new_all, state, tok_rows, tok_rows, True)
    mixed_heads = (
        (summed / row_total)
        .astype(jnp.bfloat16)
        .reshape(head_group, tok_rows, HD)
    )
    mixed_heads = jnp.transpose(mixed_heads, (1, 0, 2)).reshape(tok_rows, kv_width * head_group)
    reduced = lax.psum_scatter(
        lax.dot_general(
            out_weight, mixed_heads, (((0,), (1,)), ((), ())), preferred_element_type=jnp.float32
        ).astype(jnp.bfloat16),
        "tp",
        scatter_dimension=0,
        tiled=True,
    ).astype(jnp.float32)
    attended = reduced.T.astype(jnp.bfloat16)
    block_total = block_dest.shape[0]
    capacity = 2 * block_total // seq_count
    destination = block_dest[:, 0]
    onehot = (destination[:, None] == jnp.arange(seq_count, dtype=jnp.int32)[None, :]).astype(
        jnp.int32
    )
    earlier_count = jnp.sum((jnp.cumsum(onehot, axis=0, dtype=jnp.int32) - onehot) * onehot, axis=1)
    slot_index = destination * capacity + earlier_count
    slot_match = slot_index[None, :] == jnp.arange(seq_count * capacity, dtype=jnp.int32)[:, None]
    filled = jnp.any(slot_match, axis=1)
    source_block = jnp.sum(
        jnp.where(slot_match, jnp.arange(block_total, dtype=jnp.int32)[None, :], 0), axis=1
    )
    blocks = finished_cache.reshape(LAYERS, block_total, BLK, 2, kv_width)
    outgoing = jnp.where(
        filled[None, :, None, None, None],
        jnp.take(blocks, source_block, axis=1),
        jnp.zeros((), blocks.dtype),
    )
    outgoing = outgoing.reshape(LAYERS, seq_count, capacity * BLK, 2, kv_width)
    incoming = lax.all_to_all(outgoing, "seq", split_axis=1, concat_axis=1, tiled=True)
    page_pool = incoming.reshape(LAYERS, seq_count * capacity * BLK, 2, kv_width)
    return (attended, page_pool)


def solution(mesh):
    return jax.shard_map(
        on_device,
        mesh=mesh,
        in_specs=(
            P("seq", "tp"),
            P(),
            P(None, "tp"),
            P(None, None, "tp"),
            P("tp", None),
            P("seq", None, "tp"),
            P(),
            P(None, "seq", None, "tp"),
            P("seq", None),
        ),
        out_specs=(P("seq", "tp"), P(None, "seq", None, "tp")),
        check_vma=False,
    )
```

```python
import math
import functools

import jax
import jax.numpy as jnp
from jax import lax
from jax.experimental import pallas as pl
from jax.experimental.pallas import tpu as pltpu
from jax.sharding import PartitionSpec as P

D = 5120
HD = 128
LAYERS = 4
BLK = 16
CTX_BLOCK = 1024


rms_eps = 1e-06
rope_base = 1000000.0
neg_fill = -1e30


def rotate_pairs(values, positions):
    half_width = values.shape[-1] // 2
    frequency = jnp.exp(
        jnp.arange(half_width, dtype=jnp.float32) * (-2.0 * math.log(rope_base) / values.shape[-1])
    )
    angles = positions[:, None] * frequency[None, :]
    cosine = jnp.cos(angles)[:, None, :]
    sine_part = jnp.sin(angles)[:, None, :]
    first_half = values[..., :half_width]
    second_half = values[..., half_width:]
    return jnp.concatenate(
        [
            first_half * cosine - second_half * sine_part,
            second_half * cosine + first_half * sine_part,
        ],
        -1,
    )


def flash_kernel(
    scalars, q_ref, kv_ref, m_in, l_in, acc_in, m_ref, l_ref, acc_ref,
    *, block_rows, tok_rows, causal
):
    step = pl.program_id(0)
    span_first = scalars[0]
    seq_place = scalars[1]

    @pl.when(step == 0)
    def _():
        m_ref[...] = m_in[...]
        l_ref[...] = l_in[...]
        acc_ref[...] = acc_in[...]

    if causal:
        live = step <= seq_place
    else:
        live = step * block_rows < span_first

    @pl.when(live)
    def _():
        q = q_ref[...]
        k = kv_ref[:, :HD]
        v = kv_ref[:, HD:]
        scores = lax.dot_general(
            q, k, (((1,), (1,)), ((), ())), preferred_element_type=jnp.float32
        ) * HD ** (-0.5)
        col = lax.broadcasted_iota(jnp.int32, scores.shape, 1) + step * block_rows
        if causal:
            row = (lax.broadcasted_iota(jnp.int32, scores.shape, 0) & (tok_rows - 1)) + seq_place * tok_rows
            visible = col <= row
        else:
            visible = col < span_first
        row_max = m_ref[...]
        new_max = jnp.maximum(row_max, jnp.max(jnp.where(visible, scores, neg_fill), 1, keepdims=True))
        weights = jnp.where(visible, jnp.exp(scores - new_max), 0.0)
        rescale = jnp.exp(row_max - new_max)
        l_ref[...] = l_ref[...] * rescale + jnp.sum(weights, 1, keepdims=True)
        acc_ref[...] = acc_ref[...] * rescale + jnp.dot(
            weights.astype(jnp.bfloat16), v, preferred_element_type=jnp.float32
        )
        m_ref[...] = new_max


def flash_pass(scalars, queries, kv_rows, state, block_rows, tok_rows, causal):
    rows = queries.shape[0]
    block_count = kv_rows.shape[0] // block_rows
    if causal:
        def kv_map(j, s):
            return (jnp.minimum(j, s[1]), 0)
    else:
        def kv_map(j, s):
            last = (s[0] + block_rows - 1) // block_rows - 1
            return (jnp.maximum(jnp.minimum(j, last), 0), 0)
    full = lambda j, s: (0, 0)
    kernel = functools.partial(
        flash_kernel, block_rows=block_rows, tok_rows=tok_rows, causal=causal
    )
    return pl.pallas_call(
        kernel,
        out_shape=(
            jax.ShapeDtypeStruct((rows, 1), jnp.float32),
            jax.ShapeDtypeStruct((rows, 1), jnp.float32),
            jax.ShapeDtypeStruct((rows, HD), jnp.float32),
        ),
        grid_spec=pltpu.PrefetchScalarGridSpec(
            num_scalar_prefetch=1,
            grid=(block_count,),
            in_specs=[
                pl.BlockSpec((rows, HD), full),
                pl.BlockSpec((block_rows, 2 * HD), kv_map),
                pl.BlockSpec((rows, 1), full),
                pl.BlockSpec((rows, 1), full),
                pl.BlockSpec((rows, HD), full),
            ],
            out_specs=[
                pl.BlockSpec((rows, 1), full),
                pl.BlockSpec((rows, 1), full),
                pl.BlockSpec((rows, HD), full),
            ],
        ),
        compiler_params=pltpu.CompilerParams(
            dimension_semantics=("arbitrary",), vmem_limit_bytes=48 * 1024 * 1024
        ),
    )(scalars, queries, kv_rows, *state)


def move_pages(finished_cache, block_dest, seq_count, seq_place, kv_width):
    block_total = block_dest.shape[0]
    capacity = 2 * block_total // seq_count
    destination = (block_dest[:, 0] - seq_place) % seq_count
    onehot = (destination[:, None] == jnp.arange(seq_count, dtype=jnp.int32)[None, :]).astype(
        jnp.int32
    )
    earlier_count = jnp.sum((jnp.cumsum(onehot, axis=0, dtype=jnp.int32) - onehot) * onehot, axis=1)
    slot_index = destination * capacity + earlier_count
    slot_match = slot_index[None, :] == jnp.arange(seq_count * capacity, dtype=jnp.int32)[:, None]
    filled = jnp.any(slot_match, axis=1)
    source_block = jnp.sum(
        jnp.where(slot_match, jnp.arange(block_total, dtype=jnp.int32)[None, :], 0), axis=1
    )
    blocks = finished_cache.reshape(LAYERS, block_total, BLK, 2, kv_width)
    outgoing = jnp.where(
        filled[None, :, None, None, None],
        jnp.take(blocks, source_block, axis=1),
        jnp.zeros((), blocks.dtype),
    )
    outgoing = outgoing.reshape(LAYERS, seq_count, capacity * BLK, 2, kv_width)
    piece_rows = capacity * BLK
    page_pool = jnp.zeros((LAYERS, seq_count * piece_rows, 2, kv_width), blocks.dtype)
    for shift in range(seq_count):
        piece = outgoing[:, shift]
        if shift:
            piece = lax.ppermute(
                piece, "seq", [(s, (s + shift) % seq_count) for s in range(seq_count)]
            )
        source = (seq_place - shift) % seq_count
        page_pool = lax.dynamic_update_slice(page_pool, piece, (0, source * piece_rows, 0, 0))
    return page_pool


def on_device(
    tokens,
    norm_gain,
    q_weight,
    kv_weight,
    out_weight,
    ctx_cache,
    span_start,
    finished_cache,
    block_dest,
):
    seq_count = lax.axis_size("seq")
    seq_place = lax.axis_index("seq")
    tok_rows = tokens.shape[0]
    kv_heads = kv_weight.shape[2] // HD
    head_group = q_weight.shape[1] // HD // kv_heads
    kv_width = kv_heads * HD
    ctx_rows = ctx_cache.reshape(ctx_cache.shape[0], 2 * kv_width)
    ctx_all = lax.all_gather(ctx_rows, "seq", axis=0, tiled=True)
    page_pool = move_pages(finished_cache, block_dest, seq_count, seq_place, kv_width)
    page_pool, ctx_all = lax.optimization_barrier((page_pool, ctx_all))
    gathered = lax.all_gather(tokens, "tp", axis=1, tiled=True)
    widened = gathered.astype(jnp.float32)
    normed = (
        widened
        * lax.rsqrt(jnp.mean(widened * widened, axis=-1, keepdims=True) + rms_eps)
        * norm_gain
    ).astype(jnp.bfloat16)
    span_first = span_start[0]
    positions = (span_first + seq_place * tok_rows + jnp.arange(tok_rows, dtype=jnp.int32)).astype(
        jnp.float32
    )
    queries = jnp.dot(normed, q_weight, preferred_element_type=jnp.float32).reshape(
        tok_rows, kv_heads * head_group, HD
    )
    queries = rotate_pairs(queries, positions).astype(jnp.bfloat16)
    queries = jnp.transpose(queries, (1, 0, 2)).reshape(head_group * tok_rows, HD)
    projected = jnp.dot(
        normed, kv_weight.reshape(D, 2 * kv_width), preferred_element_type=jnp.float32
    ).reshape(tok_rows, 2, kv_heads, HD)
    new_keys = (
        rotate_pairs(projected[:, 0], positions).astype(jnp.bfloat16).reshape(tok_rows, kv_width)
    )
    new_values = projected[:, 1].astype(jnp.bfloat16).reshape(tok_rows, kv_width)
    new_rows = jnp.concatenate([new_keys, new_values], 1)
    new_all = lax.all_gather(new_rows, "seq", axis=0, tiled=True)
    query_rows = head_group * tok_rows
    scalars = jnp.stack([span_first, seq_place]).astype(jnp.int32)
    empty_state = (
        jnp.full((query_rows, 1), neg_fill, jnp.float32),
        jnp.zeros((query_rows, 1), jnp.float32),
        jnp.zeros((query_rows, HD), jnp.float32),
    )
    state = flash_pass(scalars, queries, ctx_all, empty_state, CTX_BLOCK, tok_rows, False)
    row_max, row_total, summed = flash_pass(scalars, queries, new_all, state, tok_rows, tok_rows, True)
    mixed_heads = (
        (summed / row_total)
        .astype(jnp.bfloat16)
        .reshape(head_group, tok_rows, HD)
    )
    mixed_heads = jnp.transpose(mixed_heads, (1, 0, 2)).reshape(tok_rows, kv_width * head_group)
    reduced = lax.psum_scatter(
        lax.dot_general(
            out_weight, mixed_heads, (((0,), (1,)), ((), ())), preferred_element_type=jnp.float32
        ).astype(jnp.bfloat16),
        "tp",
        scatter_dimension=0,
        tiled=True,
    ).astype(jnp.float32)
    attended = reduced.T.astype(jnp.bfloat16)
    return (attended, page_pool)


def solution(mesh):
    return jax.shard_map(
        on_device,
        mesh=mesh,
        in_specs=(
            P("seq", "tp"),
            P(),
            P(None, "tp"),
            P(None, None, "tp"),
            P("tp", None),
            P("seq", None, "tp"),
            P(),
            P(None, "seq", None, "tp"),
            P("seq", None),
        ),
        out_specs=(P("seq", "tp"), P(None, "seq", None, "tp")),
        check_vma=False,
    )
```

```python
import math
import functools

import jax
import jax.numpy as jnp
from jax import lax
from jax.experimental import pallas as pl
from jax.experimental.pallas import tpu as pltpu
from jax.sharding import PartitionSpec as P

D = 5120
HD = 128
LAYERS = 4
BLK = 16
CTX_BLOCK = 1024


rms_eps = 1e-06
rope_base = 1000000.0
neg_fill = -1e30


def rotate_pairs(values, positions):
    half_width = values.shape[-1] // 2
    frequency = jnp.exp(
        jnp.arange(half_width, dtype=jnp.float32) * (-2.0 * math.log(rope_base) / values.shape[-1])
    )
    angles = positions[:, None] * frequency[None, :]
    cosine = jnp.cos(angles)[:, None, :]
    sine_part = jnp.sin(angles)[:, None, :]
    first_half = values[..., :half_width]
    second_half = values[..., half_width:]
    return jnp.concatenate(
        [
            first_half * cosine - second_half * sine_part,
            second_half * cosine + first_half * sine_part,
        ],
        -1,
    )


def flash_kernel(
    scalars, q_ref, kv_ref, m_in, l_in, acc_in, m_ref, l_ref, acc_ref,
    *, block_rows, tok_rows, causal
):
    step = pl.program_id(0)
    span_first = scalars[0]
    seq_place = scalars[1]

    @pl.when(step == 0)
    def _():
        m_ref[...] = m_in[...]
        l_ref[...] = l_in[...]
        acc_ref[...] = acc_in[...]

    if causal:
        live = step <= seq_place
        key_first = (seq_place - step) * block_rows
    else:
        key_first = step * block_rows
        live = key_first < span_first

    @pl.when(live)
    def _():
        q = q_ref[...]
        k = kv_ref[:, :HD]
        v = kv_ref[:, HD:]
        scores = lax.dot_general(
            q, k, (((1,), (1,)), ((), ())), preferred_element_type=jnp.float32
        ) * HD ** (-0.5)
        col = lax.broadcasted_iota(jnp.int32, scores.shape, 1) + key_first
        if causal:
            row = (lax.broadcasted_iota(jnp.int32, scores.shape, 0) & (tok_rows - 1)) + seq_place * tok_rows
            visible = col <= row
        else:
            visible = col < span_first
        row_max = m_ref[...]
        new_max = jnp.maximum(row_max, jnp.max(jnp.where(visible, scores, neg_fill), 1, keepdims=True))
        weights = jnp.where(visible, jnp.exp(scores - new_max), 0.0)
        rescale = jnp.exp(row_max - new_max)
        l_ref[...] = l_ref[...] * rescale + jnp.sum(weights, 1, keepdims=True)
        acc_ref[...] = acc_ref[...] * rescale + jnp.dot(
            weights.astype(jnp.bfloat16), v, preferred_element_type=jnp.float32
        )
        m_ref[...] = new_max


def flash_pass(scalars, queries, kv_rows, state, block_rows, tok_rows, causal):
    rows = queries.shape[0]
    block_count = kv_rows.shape[0] // block_rows
    if causal:
        def kv_map(j, s):
            return (jnp.minimum(j, s[1]), 0)
    else:
        def kv_map(j, s):
            last = (s[0] + block_rows - 1) // block_rows - 1
            return (jnp.maximum(jnp.minimum(j, last), 0), 0)
    full = lambda j, s: (0, 0)
    kernel = functools.partial(
        flash_kernel, block_rows=block_rows, tok_rows=tok_rows, causal=causal
    )
    return pl.pallas_call(
        kernel,
        out_shape=(
            jax.ShapeDtypeStruct((rows, 1), jnp.float32),
            jax.ShapeDtypeStruct((rows, 1), jnp.float32),
            jax.ShapeDtypeStruct((rows, HD), jnp.float32),
        ),
        grid_spec=pltpu.PrefetchScalarGridSpec(
            num_scalar_prefetch=1,
            grid=(block_count,),
            in_specs=[
                pl.BlockSpec((rows, HD), full),
                pl.BlockSpec((block_rows, 2 * HD), kv_map),
                pl.BlockSpec((rows, 1), full),
                pl.BlockSpec((rows, 1), full),
                pl.BlockSpec((rows, HD), full),
            ],
            out_specs=[
                pl.BlockSpec((rows, 1), full),
                pl.BlockSpec((rows, 1), full),
                pl.BlockSpec((rows, HD), full),
            ],
        ),
        compiler_params=pltpu.CompilerParams(
            dimension_semantics=("arbitrary",), vmem_limit_bytes=48 * 1024 * 1024
        ),
    )(scalars, queries, kv_rows, *state)


def move_pages(finished_cache, block_dest, seq_count, seq_place, kv_width):
    block_total = block_dest.shape[0]
    capacity = 2 * block_total // seq_count
    destination = (block_dest[:, 0] - seq_place) % seq_count
    onehot = (destination[:, None] == jnp.arange(seq_count, dtype=jnp.int32)[None, :]).astype(
        jnp.int32
    )
    earlier_count = jnp.sum((jnp.cumsum(onehot, axis=0, dtype=jnp.int32) - onehot) * onehot, axis=1)
    slot_index = destination * capacity + earlier_count
    slot_match = slot_index[None, :] == jnp.arange(seq_count * capacity, dtype=jnp.int32)[:, None]
    filled = jnp.any(slot_match, axis=1)
    source_block = jnp.sum(
        jnp.where(slot_match, jnp.arange(block_total, dtype=jnp.int32)[None, :], 0), axis=1
    )
    blocks = finished_cache.reshape(LAYERS, block_total, BLK, 2, kv_width)
    outgoing = jnp.where(
        filled[None, :, None, None, None],
        jnp.take(blocks, source_block, axis=1),
        jnp.zeros((), blocks.dtype),
    )
    outgoing = outgoing.reshape(LAYERS, seq_count, capacity * BLK, 2, kv_width)
    piece_rows = capacity * BLK
    page_pool = jnp.zeros((LAYERS, seq_count * piece_rows, 2, kv_width), blocks.dtype)
    for shift in range(seq_count):
        piece = outgoing[:, shift]
        if shift:
            piece = lax.ppermute(
                piece, "seq", [(s, (s + shift) % seq_count) for s in range(seq_count)]
            )
        source = (seq_place - shift) % seq_count
        page_pool = lax.dynamic_update_slice(page_pool, piece, (0, source * piece_rows, 0, 0))
    return page_pool


def on_device(
    tokens,
    norm_gain,
    q_weight,
    kv_weight,
    out_weight,
    ctx_cache,
    span_start,
    finished_cache,
    block_dest,
):
    seq_count = lax.axis_size("seq")
    seq_place = lax.axis_index("seq")
    tok_rows = tokens.shape[0]
    kv_heads = kv_weight.shape[2] // HD
    head_group = q_weight.shape[1] // HD // kv_heads
    kv_width = kv_heads * HD
    ctx_rows = ctx_cache.reshape(ctx_cache.shape[0], 2 * kv_width)
    ctx_all = lax.all_gather(ctx_rows, "seq", axis=0, tiled=True)
    page_pool = move_pages(finished_cache, block_dest, seq_count, seq_place, kv_width)
    page_pool, ctx_all = lax.optimization_barrier((page_pool, ctx_all))
    gathered = lax.all_gather(tokens, "tp", axis=1, tiled=True)
    widened = gathered.astype(jnp.float32)
    normed = (
        widened
        * lax.rsqrt(jnp.mean(widened * widened, axis=-1, keepdims=True) + rms_eps)
        * norm_gain
    ).astype(jnp.bfloat16)
    span_first = span_start[0]
    positions = (span_first + seq_place * tok_rows + jnp.arange(tok_rows, dtype=jnp.int32)).astype(
        jnp.float32
    )
    queries = jnp.dot(normed, q_weight, preferred_element_type=jnp.float32).reshape(
        tok_rows, kv_heads * head_group, HD
    )
    queries = rotate_pairs(queries, positions).astype(jnp.bfloat16)
    queries = jnp.transpose(queries, (1, 0, 2)).reshape(head_group * tok_rows, HD)
    projected = jnp.dot(
        normed, kv_weight.reshape(D, 2 * kv_width), preferred_element_type=jnp.float32
    ).reshape(tok_rows, 2, kv_heads, HD)
    new_keys = (
        rotate_pairs(projected[:, 0], positions).astype(jnp.bfloat16).reshape(tok_rows, kv_width)
    )
    new_values = projected[:, 1].astype(jnp.bfloat16).reshape(tok_rows, kv_width)
    new_rows = jnp.concatenate([new_keys, new_values], 1)
    arrived = [new_rows]
    for shift in range(1, seq_count):
        arrived.append(
            lax.ppermute(new_rows, "seq", [(s, s + shift) for s in range(seq_count - shift)])
        )
    new_all = jnp.concatenate(arrived, 0)
    query_rows = head_group * tok_rows
    scalars = jnp.stack([span_first, seq_place]).astype(jnp.int32)
    empty_state = (
        jnp.full((query_rows, 1), neg_fill, jnp.float32),
        jnp.zeros((query_rows, 1), jnp.float32),
        jnp.zeros((query_rows, HD), jnp.float32),
    )
    state = flash_pass(scalars, queries, ctx_all, empty_state, CTX_BLOCK, tok_rows, False)
    row_max, row_total, summed = flash_pass(scalars, queries, new_all, state, tok_rows, tok_rows, True)
    mixed_heads = (
        (summed / row_total)
        .astype(jnp.bfloat16)
        .reshape(head_group, tok_rows, HD)
    )
    mixed_heads = jnp.transpose(mixed_heads, (1, 0, 2)).reshape(tok_rows, kv_width * head_group)
    tp_count = lax.axis_size("tp")
    tp_place = lax.axis_index("tp")
    out_cols = out_weight.shape[1] // tp_count
    partial = jnp.dot(mixed_heads, out_weight, preferred_element_type=jnp.float32)
    reduced = lax.dynamic_slice_in_dim(partial, tp_place * out_cols, out_cols, 1)
    partial = partial.astype(jnp.bfloat16)
    for shift in range(1, tp_count):
        chunk = lax.dynamic_slice_in_dim(
            partial, ((tp_place + shift) % tp_count) * out_cols, out_cols, 1
        )
        reduced = reduced + lax.ppermute(
            chunk, "tp", [(i, (i + shift) % tp_count) for i in range(tp_count)]
        ).astype(jnp.float32)
    attended = reduced.astype(jnp.bfloat16)
    return (attended, page_pool)


def solution(mesh):
    return jax.shard_map(
        on_device,
        mesh=mesh,
        in_specs=(
            P("seq", "tp"),
            P(),
            P(None, "tp"),
            P(None, None, "tp"),
            P("tp", None),
            P("seq", None, "tp"),
            P(),
            P(None, "seq", None, "tp"),
            P("seq", None),
        ),
        out_specs=(P("seq", "tp"), P(None, "seq", None, "tp")),
        check_vma=False,
    )
```

```python
import math
import functools

import jax
import jax.numpy as jnp
from jax import lax
from jax.experimental import pallas as pl
from jax.experimental.pallas import tpu as pltpu
from jax.sharding import PartitionSpec as P

D = 5120
HD = 128
LAYERS = 4
BLK = 16
CTX_BLOCK = 1024


rms_eps = 1e-06
rope_base = 1000000.0
neg_fill = -1e30


def rotate_pairs(values, positions):
    half_width = values.shape[-1] // 2
    frequency = jnp.exp(
        jnp.arange(half_width, dtype=jnp.float32) * (-2.0 * math.log(rope_base) / values.shape[-1])
    )
    angles = positions[:, None] * frequency[None, :]
    cosine = jnp.cos(angles)[:, None, :]
    sine_part = jnp.sin(angles)[:, None, :]
    first_half = values[..., :half_width]
    second_half = values[..., half_width:]
    return jnp.concatenate(
        [
            first_half * cosine - second_half * sine_part,
            second_half * cosine + first_half * sine_part,
        ],
        -1,
    )


def flash_kernel(
    scalars, q_ref, kv_ref, m_in, l_in, acc_in, m_ref, l_ref, acc_ref,
    *, block_rows, tok_rows, causal
):
    step = pl.program_id(0)
    span_first = scalars[0]
    seq_place = scalars[1]

    @pl.when(step == 0)
    def _():
        m_ref[...] = m_in[...]
        l_ref[...] = l_in[...]
        acc_ref[...] = acc_in[...]

    if causal:
        group = block_rows // tok_rows
        live = step * group <= seq_place
    else:
        key_first = step * block_rows
        live = key_first < span_first

    @pl.when(live)
    def _():
        q = q_ref[...]
        k = kv_ref[:, :HD]
        v = kv_ref[:, HD:]
        scores = lax.dot_general(
            q, k, (((1,), (1,)), ((), ())), preferred_element_type=jnp.float32
        ) * HD ** (-0.5)
        col = lax.broadcasted_iota(jnp.int32, scores.shape, 1)
        if causal:
            shift = tok_rows.bit_length() - 1
            distance = lax.shift_right_logical(col, shift) + step * group
            row = lax.broadcasted_iota(jnp.int32, scores.shape, 0) & (tok_rows - 1)
            visible = (distance <= seq_place) & (
                (distance > 0) | ((col & (tok_rows - 1)) <= row)
            )
        else:
            visible = col + key_first < span_first
        row_max = m_ref[...]
        new_max = jnp.maximum(row_max, jnp.max(jnp.where(visible, scores, neg_fill), 1, keepdims=True))
        weights = jnp.where(visible, jnp.exp(scores - new_max), 0.0)
        rescale = jnp.exp(row_max - new_max)
        l_ref[...] = l_ref[...] * rescale + jnp.sum(weights, 1, keepdims=True)
        acc_ref[...] = acc_ref[...] * rescale + jnp.dot(
            weights.astype(jnp.bfloat16), v, preferred_element_type=jnp.float32
        )
        m_ref[...] = new_max


def flash_pass(scalars, queries, kv_rows, state, block_rows, tok_rows, causal):
    rows = queries.shape[0]
    block_count = kv_rows.shape[0] // block_rows
    if causal:
        def kv_map(j, s):
            return (jnp.minimum(j, s[1] // (block_rows // tok_rows)), 0)
    else:
        def kv_map(j, s):
            last = (s[0] + block_rows - 1) // block_rows - 1
            return (jnp.maximum(jnp.minimum(j, last), 0), 0)
    full = lambda j, s: (0, 0)
    kernel = functools.partial(
        flash_kernel, block_rows=block_rows, tok_rows=tok_rows, causal=causal
    )
    return pl.pallas_call(
        kernel,
        out_shape=(
            jax.ShapeDtypeStruct((rows, 1), jnp.float32),
            jax.ShapeDtypeStruct((rows, 1), jnp.float32),
            jax.ShapeDtypeStruct((rows, HD), jnp.float32),
        ),
        grid_spec=pltpu.PrefetchScalarGridSpec(
            num_scalar_prefetch=1,
            grid=(block_count,),
            in_specs=[
                pl.BlockSpec((rows, HD), full),
                pl.BlockSpec((block_rows, 2 * HD), kv_map),
                pl.BlockSpec((rows, 1), full),
                pl.BlockSpec((rows, 1), full),
                pl.BlockSpec((rows, HD), full),
            ],
            out_specs=[
                pl.BlockSpec((rows, 1), full),
                pl.BlockSpec((rows, 1), full),
                pl.BlockSpec((rows, HD), full),
            ],
        ),
        compiler_params=pltpu.CompilerParams(
            dimension_semantics=("arbitrary",), vmem_limit_bytes=48 * 1024 * 1024
        ),
        cost_estimate=pl.CostEstimate(
            flops=4 * rows * HD * kv_rows.shape[0],
            transcendentals=rows * kv_rows.shape[0],
            bytes_accessed=kv_rows.size * 2 + rows * HD * 6,
        ),
    )(scalars, queries, kv_rows, *state)


def move_pages(finished_cache, block_dest, seq_count, seq_place, kv_width):
    block_total = block_dest.shape[0]
    capacity = 2 * block_total // seq_count
    destination = (block_dest[:, 0] - seq_place) % seq_count
    onehot = (destination[:, None] == jnp.arange(seq_count, dtype=jnp.int32)[None, :]).astype(
        jnp.int32
    )
    earlier_count = jnp.sum((jnp.cumsum(onehot, axis=0, dtype=jnp.int32) - onehot) * onehot, axis=1)
    slot_index = destination * capacity + earlier_count
    slot_match = slot_index[None, :] == jnp.arange(seq_count * capacity, dtype=jnp.int32)[:, None]
    filled = jnp.any(slot_match, axis=1)
    source_block = jnp.sum(
        jnp.where(slot_match, jnp.arange(block_total, dtype=jnp.int32)[None, :], 0), axis=1
    )
    blocks = finished_cache.reshape(LAYERS, block_total, BLK, 2, kv_width)
    outgoing = jnp.where(
        filled[None, :, None, None, None],
        jnp.take(blocks, source_block, axis=1),
        jnp.zeros((), blocks.dtype),
    )
    outgoing = outgoing.reshape(LAYERS, seq_count, capacity * BLK, 2, kv_width)
    piece_rows = capacity * BLK
    page_pool = jnp.zeros((LAYERS, seq_count * piece_rows, 2, kv_width), blocks.dtype)
    for shift in range(seq_count):
        piece = outgoing[:, shift]
        if shift:
            piece = lax.ppermute(
                piece, "seq", [(s, (s + shift) % seq_count) for s in range(seq_count)]
            )
        source = (seq_place - shift) % seq_count
        page_pool = lax.dynamic_update_slice(page_pool, piece, (0, source * piece_rows, 0, 0))
    return page_pool


def on_device(
    tokens,
    norm_gain,
    q_weight,
    kv_weight,
    out_weight,
    ctx_cache,
    span_start,
    finished_cache,
    block_dest,
):
    seq_count = lax.axis_size("seq")
    seq_place = lax.axis_index("seq")
    tok_rows = tokens.shape[0]
    kv_heads = kv_weight.shape[2] // HD
    head_group = q_weight.shape[1] // HD // kv_heads
    kv_width = kv_heads * HD
    ctx_rows = ctx_cache.reshape(ctx_cache.shape[0], 2 * kv_width)
    ctx_all = lax.all_gather(ctx_rows, "seq", axis=0, tiled=True)
    page_pool = move_pages(finished_cache, block_dest, seq_count, seq_place, kv_width)
    gathered = lax.all_gather(tokens, "tp", axis=1, tiled=True)
    widened = gathered.astype(jnp.float32)
    normed = (
        widened
        * lax.rsqrt(jnp.mean(widened * widened, axis=-1, keepdims=True) + rms_eps)
        * norm_gain
    ).astype(jnp.bfloat16)
    span_first = span_start[0]
    positions = (span_first + seq_place * tok_rows + jnp.arange(tok_rows, dtype=jnp.int32)).astype(
        jnp.float32
    )
    queries = jnp.dot(normed, q_weight, preferred_element_type=jnp.float32).reshape(
        tok_rows, kv_heads * head_group, HD
    )
    queries = rotate_pairs(queries, positions).astype(jnp.bfloat16)
    queries = jnp.transpose(queries, (1, 0, 2)).reshape(head_group * tok_rows, HD)
    projected = jnp.dot(
        normed, kv_weight.reshape(D, 2 * kv_width), preferred_element_type=jnp.float32
    ).reshape(tok_rows, 2, kv_heads, HD)
    new_keys = (
        rotate_pairs(projected[:, 0], positions).astype(jnp.bfloat16).reshape(tok_rows, kv_width)
    )
    new_values = projected[:, 1].astype(jnp.bfloat16).reshape(tok_rows, kv_width)
    new_rows = jnp.concatenate([new_keys, new_values], 1)
    arrived = [new_rows]
    for shift in range(1, seq_count):
        arrived.append(
            lax.ppermute(new_rows, "seq", [(s, s + shift) for s in range(seq_count - shift)])
        )
    new_all = jnp.concatenate(arrived, 0)
    query_rows = head_group * tok_rows
    scalars = jnp.stack([span_first, seq_place]).astype(jnp.int32)
    empty_state = (
        jnp.full((query_rows, 1), neg_fill, jnp.float32),
        jnp.zeros((query_rows, 1), jnp.float32),
        jnp.zeros((query_rows, HD), jnp.float32),
    )
    state = flash_pass(scalars, queries, ctx_all, empty_state, CTX_BLOCK, tok_rows, False)
    page_pool, state = lax.optimization_barrier((page_pool, state))
    row_max, row_total, summed = flash_pass(scalars, queries, new_all, state, CTX_BLOCK, tok_rows, True)
    mixed_heads = (
        (summed / row_total)
        .astype(jnp.bfloat16)
        .reshape(head_group, tok_rows, HD)
    )
    mixed_heads = jnp.transpose(mixed_heads, (1, 0, 2)).reshape(tok_rows, kv_width * head_group)
    tp_count = lax.axis_size("tp")
    tp_place = lax.axis_index("tp")
    out_cols = out_weight.shape[1] // tp_count
    partial = jnp.dot(mixed_heads, out_weight, preferred_element_type=jnp.float32)
    reduced = lax.dynamic_slice_in_dim(partial, tp_place * out_cols, out_cols, 1)
    partial = partial.astype(jnp.bfloat16)
    for shift in range(1, tp_count):
        chunk = lax.dynamic_slice_in_dim(
            partial, ((tp_place + shift) % tp_count) * out_cols, out_cols, 1
        )
        reduced = reduced + lax.ppermute(
            chunk, "tp", [(i, (i + shift) % tp_count) for i in range(tp_count)]
        ).astype(jnp.float32)
    attended = reduced.astype(jnp.bfloat16)
    return (attended, page_pool)


def solution(mesh):
    return jax.shard_map(
        on_device,
        mesh=mesh,
        in_specs=(
            P("seq", "tp"),
            P(),
            P(None, "tp"),
            P(None, None, "tp"),
            P("tp", None),
            P("seq", None, "tp"),
            P(),
            P(None, "seq", None, "tp"),
            P("seq", None),
        ),
        out_specs=(P("seq", "tp"), P(None, "seq", None, "tp")),
        check_vma=False,
    )
```

```python
import math
import functools

import jax
import jax.numpy as jnp
from jax import lax
from jax.experimental import pallas as pl
from jax.experimental.pallas import tpu as pltpu
from jax.sharding import PartitionSpec as P

D = 5120
HD = 128
LAYERS = 4
BLK = 16
CTX_BLOCK = 1024


rms_eps = 1e-06
rope_base = 1000000.0
neg_fill = -1e30


def rotate_pairs(values, positions):
    half_width = values.shape[-1] // 2
    frequency = jnp.exp(
        jnp.arange(half_width, dtype=jnp.float32) * (-2.0 * math.log(rope_base) / values.shape[-1])
    )
    angles = positions[:, None] * frequency[None, :]
    cosine = jnp.cos(angles)[:, None, :]
    sine_part = jnp.sin(angles)[:, None, :]
    first_half = values[..., :half_width]
    second_half = values[..., half_width:]
    return jnp.concatenate(
        [
            first_half * cosine - second_half * sine_part,
            second_half * cosine + first_half * sine_part,
        ],
        -1,
    )


def flash_kernel(
    scalars, q_ref, kv_ref, m_in, l_in, acc_in, m_ref, l_ref, acc_ref,
    *, block_rows, tok_rows, causal
):
    step = pl.program_id(0)
    span_first = scalars[0]
    seq_place = scalars[1]

    @pl.when(step == 0)
    def _():
        m_ref[...] = m_in[...]
        l_ref[...] = l_in[...]
        acc_ref[...] = acc_in[...]

    if causal:
        group = block_rows // tok_rows
        live = step * group <= seq_place
        whole = (step > 0) & (step * group + group - 1 <= seq_place)
    else:
        key_first = step * block_rows
        live = key_first < span_first
        whole = key_first + block_rows <= span_first

    def update(masked):
        q = q_ref[...]
        k = kv_ref[:, :HD]
        v = kv_ref[:, HD:]
        scores = lax.dot_general(
            q, k, (((1,), (1,)), ((), ())), preferred_element_type=jnp.float32
        ) * HD ** (-0.5)
        row_max = m_ref[...]
        if masked:
            col = lax.broadcasted_iota(jnp.int32, scores.shape, 1)
            if causal:
                shift = tok_rows.bit_length() - 1
                distance = lax.shift_right_logical(col, shift) + step * group
                row = lax.broadcasted_iota(jnp.int32, scores.shape, 0) & (tok_rows - 1)
                visible = (distance <= seq_place) & (
                    (distance > 0) | ((col & (tok_rows - 1)) <= row)
                )
            else:
                visible = col + key_first < span_first
            new_max = jnp.maximum(
                row_max, jnp.max(jnp.where(visible, scores, neg_fill), 1, keepdims=True)
            )
            weights = jnp.where(visible, jnp.exp(scores - new_max), 0.0)
        else:
            new_max = jnp.maximum(row_max, jnp.max(scores, 1, keepdims=True))
            weights = jnp.exp(scores - new_max)
        rescale = jnp.exp(row_max - new_max)
        l_ref[...] = l_ref[...] * rescale + jnp.sum(weights, 1, keepdims=True)
        acc_ref[...] = acc_ref[...] * rescale + jnp.dot(
            weights.astype(jnp.bfloat16), v, preferred_element_type=jnp.float32
        )
        m_ref[...] = new_max

    @pl.when(whole)
    def _():
        update(False)

    @pl.when(live & jnp.logical_not(whole))
    def _():
        update(True)


def flash_pass(scalars, queries, kv_rows, state, block_rows, tok_rows, causal):
    rows = queries.shape[0]
    block_count = kv_rows.shape[0] // block_rows
    if causal:
        def kv_map(j, s):
            return (jnp.minimum(j, s[1] // (block_rows // tok_rows)), 0)
    else:
        def kv_map(j, s):
            last = (s[0] + block_rows - 1) // block_rows - 1
            return (jnp.maximum(jnp.minimum(j, last), 0), 0)
    full = lambda j, s: (0, 0)
    kernel = functools.partial(
        flash_kernel, block_rows=block_rows, tok_rows=tok_rows, causal=causal
    )
    return pl.pallas_call(
        kernel,
        out_shape=(
            jax.ShapeDtypeStruct((rows, 1), jnp.float32),
            jax.ShapeDtypeStruct((rows, 1), jnp.float32),
            jax.ShapeDtypeStruct((rows, HD), jnp.float32),
        ),
        grid_spec=pltpu.PrefetchScalarGridSpec(
            num_scalar_prefetch=1,
            grid=(block_count,),
            in_specs=[
                pl.BlockSpec((rows, HD), full),
                pl.BlockSpec((block_rows, 2 * HD), kv_map),
                pl.BlockSpec((rows, 1), full),
                pl.BlockSpec((rows, 1), full),
                pl.BlockSpec((rows, HD), full),
            ],
            out_specs=[
                pl.BlockSpec((rows, 1), full),
                pl.BlockSpec((rows, 1), full),
                pl.BlockSpec((rows, HD), full),
            ],
        ),
        compiler_params=pltpu.CompilerParams(
            dimension_semantics=("arbitrary",), vmem_limit_bytes=48 * 1024 * 1024
        ),
        cost_estimate=pl.CostEstimate(
            flops=4 * rows * HD * kv_rows.shape[0],
            transcendentals=rows * kv_rows.shape[0],
            bytes_accessed=kv_rows.size * 2 + rows * HD * 6,
        ),
    )(scalars, queries, kv_rows, *state)


def move_pages(finished_cache, block_dest, seq_count, seq_place, kv_width):
    block_total = block_dest.shape[0]
    capacity = 2 * block_total // seq_count
    destination = (block_dest[:, 0] - seq_place) % seq_count
    onehot = (destination[:, None] == jnp.arange(seq_count, dtype=jnp.int32)[None, :]).astype(
        jnp.int32
    )
    earlier_count = jnp.sum((jnp.cumsum(onehot, axis=0, dtype=jnp.int32) - onehot) * onehot, axis=1)
    slot_index = destination * capacity + earlier_count
    slot_match = slot_index[None, :] == jnp.arange(seq_count * capacity, dtype=jnp.int32)[:, None]
    filled = jnp.any(slot_match, axis=1)
    source_block = jnp.sum(
        jnp.where(slot_match, jnp.arange(block_total, dtype=jnp.int32)[None, :], 0), axis=1
    )
    blocks = finished_cache.reshape(LAYERS, block_total, BLK, 2, kv_width)
    outgoing = jnp.where(
        filled[None, :, None, None, None],
        jnp.take(blocks, source_block, axis=1),
        jnp.zeros((), blocks.dtype),
    )
    outgoing = outgoing.reshape(LAYERS, seq_count, capacity * BLK, 2, kv_width)
    piece_rows = capacity * BLK
    page_pool = jnp.zeros((LAYERS, seq_count * piece_rows, 2, kv_width), blocks.dtype)
    for shift in range(seq_count):
        piece = outgoing[:, shift]
        if shift:
            piece = lax.ppermute(
                piece, "seq", [(s, (s + shift) % seq_count) for s in range(seq_count)]
            )
        source = (seq_place - shift) % seq_count
        page_pool = lax.dynamic_update_slice(page_pool, piece, (0, source * piece_rows, 0, 0))
    return page_pool


def on_device(
    tokens,
    norm_gain,
    q_weight,
    kv_weight,
    out_weight,
    ctx_cache,
    span_start,
    finished_cache,
    block_dest,
):
    seq_count = lax.axis_size("seq")
    seq_place = lax.axis_index("seq")
    tok_rows = tokens.shape[0]
    kv_heads = kv_weight.shape[2] // HD
    head_group = q_weight.shape[1] // HD // kv_heads
    kv_width = kv_heads * HD
    ctx_rows = ctx_cache.reshape(ctx_cache.shape[0], 2 * kv_width)
    ctx_all = lax.all_gather(ctx_rows, "seq", axis=0, tiled=True)
    page_pool = move_pages(finished_cache, block_dest, seq_count, seq_place, kv_width)
    gathered = lax.all_gather(tokens, "tp", axis=1, tiled=True)
    widened = gathered.astype(jnp.float32)
    normed = (
        widened
        * lax.rsqrt(jnp.mean(widened * widened, axis=-1, keepdims=True) + rms_eps)
        * norm_gain
    ).astype(jnp.bfloat16)
    span_first = span_start[0]
    positions = (span_first + seq_place * tok_rows + jnp.arange(tok_rows, dtype=jnp.int32)).astype(
        jnp.float32
    )
    queries = jnp.dot(normed, q_weight, preferred_element_type=jnp.float32).reshape(
        tok_rows, kv_heads * head_group, HD
    )
    queries = rotate_pairs(queries, positions).astype(jnp.bfloat16)
    queries = jnp.transpose(queries, (1, 0, 2)).reshape(head_group * tok_rows, HD)
    projected = jnp.dot(
        normed, kv_weight.reshape(D, 2 * kv_width), preferred_element_type=jnp.float32
    ).reshape(tok_rows, 2, kv_heads, HD)
    new_keys = (
        rotate_pairs(projected[:, 0], positions).astype(jnp.bfloat16).reshape(tok_rows, kv_width)
    )
    new_values = projected[:, 1].astype(jnp.bfloat16).reshape(tok_rows, kv_width)
    new_rows = jnp.concatenate([new_keys, new_values], 1)
    arrived = [new_rows]
    for shift in range(1, seq_count):
        arrived.append(
            lax.ppermute(new_rows, "seq", [(s, s + shift) for s in range(seq_count - shift)])
        )
    new_all = jnp.concatenate(arrived, 0)
    query_rows = head_group * tok_rows
    scalars = jnp.stack([span_first, seq_place]).astype(jnp.int32)
    empty_state = (
        jnp.full((query_rows, 1), neg_fill, jnp.float32),
        jnp.zeros((query_rows, 1), jnp.float32),
        jnp.zeros((query_rows, HD), jnp.float32),
    )
    state = flash_pass(scalars, queries, ctx_all, empty_state, CTX_BLOCK, tok_rows, False)
    page_pool, state = lax.optimization_barrier((page_pool, state))
    row_max, row_total, summed = flash_pass(scalars, queries, new_all, state, CTX_BLOCK, tok_rows, True)
    mixed_heads = (
        (summed / row_total)
        .astype(jnp.bfloat16)
        .reshape(head_group, tok_rows, HD)
    )
    mixed_heads = jnp.transpose(mixed_heads, (1, 0, 2)).reshape(tok_rows, kv_width * head_group)
    tp_count = lax.axis_size("tp")
    tp_place = lax.axis_index("tp")
    out_cols = out_weight.shape[1] // tp_count
    partial = jnp.dot(mixed_heads, out_weight, preferred_element_type=jnp.float32)
    reduced = lax.dynamic_slice_in_dim(partial, tp_place * out_cols, out_cols, 1)
    partial = partial.astype(jnp.bfloat16)
    for shift in range(1, tp_count):
        chunk = lax.dynamic_slice_in_dim(
            partial, ((tp_place + shift) % tp_count) * out_cols, out_cols, 1
        )
        reduced = reduced + lax.ppermute(
            chunk, "tp", [(i, (i + shift) % tp_count) for i in range(tp_count)]
        ).astype(jnp.float32)
    attended = reduced.astype(jnp.bfloat16)
    return (attended, page_pool)


def solution(mesh):
    return jax.shard_map(
        on_device,
        mesh=mesh,
        in_specs=(
            P("seq", "tp"),
            P(),
            P(None, "tp"),
            P(None, None, "tp"),
            P("tp", None),
            P("seq", None, "tp"),
            P(),
            P(None, "seq", None, "tp"),
            P("seq", None),
        ),
        out_specs=(P("seq", "tp"), P(None, "seq", None, "tp")),
        check_vma=False,
    )
```

```python
import math
import functools

import jax
import jax.numpy as jnp
from jax import lax
from jax.experimental import pallas as pl
from jax.experimental.pallas import tpu as pltpu
from jax.sharding import PartitionSpec as P

D = 5120
HD = 128
LAYERS = 4
BLK = 16
CTX_BLOCK = 1024
ROW_CHUNK = 128


rms_eps = 1e-06
rope_base = 1000000.0
neg_fill = -1e30


def rotate_pairs(values, positions):
    half_width = values.shape[-1] // 2
    frequency = jnp.exp(
        jnp.arange(half_width, dtype=jnp.float32) * (-2.0 * math.log(rope_base) / values.shape[-1])
    )
    angles = positions[:, None] * frequency[None, :]
    cosine = jnp.cos(angles)[:, None, :]
    sine_part = jnp.sin(angles)[:, None, :]
    first_half = values[..., :half_width]
    second_half = values[..., half_width:]
    return jnp.concatenate(
        [
            first_half * cosine - second_half * sine_part,
            second_half * cosine + first_half * sine_part,
        ],
        -1,
    )


def flash_kernel(
    scalars, q_ref, kv_ref, m_in, l_in, acc_in, m_ref, l_ref, acc_ref,
    *, block_rows, tok_rows, causal
):
    step = pl.program_id(0)
    span_first = scalars[0]
    seq_place = scalars[1]

    @pl.when(step == 0)
    def _():
        m_ref[...] = m_in[...]
        l_ref[...] = l_in[...]
        acc_ref[...] = acc_in[...]

    if causal:
        group = block_rows // tok_rows
        live = step * group <= seq_place
    else:
        key_first = step * block_rows
        live = key_first < span_first

    @pl.when(live)
    def _():
        k = kv_ref[:, :HD]
        v = kv_ref[:, HD:]

        def chunk_step(chunk, carry):
            rows = pl.ds(pl.multiple_of(chunk * ROW_CHUNK, ROW_CHUNK), ROW_CHUNK)
            scores = lax.dot_general(
                q_ref[rows, :], k, (((1,), (1,)), ((), ())), preferred_element_type=jnp.float32
            ) * HD ** (-0.5)
            col = lax.broadcasted_iota(jnp.int32, scores.shape, 1)
            if causal:
                shift = tok_rows.bit_length() - 1
                distance = lax.shift_right_logical(col, shift) + step * group
                row = (lax.broadcasted_iota(jnp.int32, scores.shape, 0) + chunk * ROW_CHUNK) & (
                    tok_rows - 1
                )
                visible = (distance <= seq_place) & (
                    (distance > 0) | ((col & (tok_rows - 1)) <= row)
                )
            else:
                visible = col + key_first < span_first
            row_max = m_ref[rows, :]
            new_max = jnp.maximum(
                row_max, jnp.max(jnp.where(visible, scores, neg_fill), 1, keepdims=True)
            )
            weights = jnp.where(visible, jnp.exp(scores - new_max), 0.0)
            rescale = jnp.exp(row_max - new_max)
            l_ref[rows, :] = l_ref[rows, :] * rescale + jnp.sum(weights, 1, keepdims=True)
            acc_ref[rows, :] = acc_ref[rows, :] * rescale + jnp.dot(
                weights.astype(jnp.bfloat16), v, preferred_element_type=jnp.float32
            )
            m_ref[rows, :] = new_max
            return carry

        lax.fori_loop(0, q_ref.shape[0] // ROW_CHUNK, chunk_step, 0)


def flash_pass(scalars, queries, kv_rows, state, block_rows, tok_rows, causal):
    rows = queries.shape[0]
    block_count = kv_rows.shape[0] // block_rows
    if causal:
        def kv_map(j, s):
            return (jnp.minimum(j, s[1] // (block_rows // tok_rows)), 0)
    else:
        def kv_map(j, s):
            last = (s[0] + block_rows - 1) // block_rows - 1
            return (jnp.maximum(jnp.minimum(j, last), 0), 0)
    full = lambda j, s: (0, 0)
    kernel = functools.partial(
        flash_kernel, block_rows=block_rows, tok_rows=tok_rows, causal=causal
    )
    return pl.pallas_call(
        kernel,
        out_shape=(
            jax.ShapeDtypeStruct((rows, 1), jnp.float32),
            jax.ShapeDtypeStruct((rows, 1), jnp.float32),
            jax.ShapeDtypeStruct((rows, HD), jnp.float32),
        ),
        grid_spec=pltpu.PrefetchScalarGridSpec(
            num_scalar_prefetch=1,
            grid=(block_count,),
            in_specs=[
                pl.BlockSpec((rows, HD), full),
                pl.BlockSpec((block_rows, 2 * HD), kv_map),
                pl.BlockSpec((rows, 1), full),
                pl.BlockSpec((rows, 1), full),
                pl.BlockSpec((rows, HD), full),
            ],
            out_specs=[
                pl.BlockSpec((rows, 1), full),
                pl.BlockSpec((rows, 1), full),
                pl.BlockSpec((rows, HD), full),
            ],
        ),
        compiler_params=pltpu.CompilerParams(
            dimension_semantics=("arbitrary",), vmem_limit_bytes=48 * 1024 * 1024
        ),
        cost_estimate=pl.CostEstimate(
            flops=4 * rows * HD * kv_rows.shape[0],
            transcendentals=rows * kv_rows.shape[0],
            bytes_accessed=kv_rows.size * 2 + rows * HD * 6,
        ),
    )(scalars, queries, kv_rows, *state)


def move_pages(finished_cache, block_dest, seq_count, seq_place, kv_width):
    block_total = block_dest.shape[0]
    capacity = 2 * block_total // seq_count
    destination = (block_dest[:, 0] - seq_place) % seq_count
    onehot = (destination[:, None] == jnp.arange(seq_count, dtype=jnp.int32)[None, :]).astype(
        jnp.int32
    )
    earlier_count = jnp.sum((jnp.cumsum(onehot, axis=0, dtype=jnp.int32) - onehot) * onehot, axis=1)
    slot_index = destination * capacity + earlier_count
    slot_match = slot_index[None, :] == jnp.arange(seq_count * capacity, dtype=jnp.int32)[:, None]
    filled = jnp.any(slot_match, axis=1)
    source_block = jnp.sum(
        jnp.where(slot_match, jnp.arange(block_total, dtype=jnp.int32)[None, :], 0), axis=1
    )
    blocks = finished_cache.reshape(LAYERS, block_total, BLK, 2, kv_width)
    outgoing = jnp.where(
        filled[None, :, None, None, None],
        jnp.take(blocks, source_block, axis=1),
        jnp.zeros((), blocks.dtype),
    )
    outgoing = outgoing.reshape(LAYERS, seq_count, capacity * BLK, 2, kv_width)
    piece_rows = capacity * BLK
    page_pool = jnp.zeros((LAYERS, seq_count * piece_rows, 2, kv_width), blocks.dtype)
    for shift in range(seq_count):
        piece = outgoing[:, shift]
        if shift:
            piece = lax.ppermute(
                piece, "seq", [(s, (s + shift) % seq_count) for s in range(seq_count)]
            )
        source = (seq_place - shift) % seq_count
        page_pool = lax.dynamic_update_slice(page_pool, piece, (0, source * piece_rows, 0, 0))
    return page_pool


def on_device(
    tokens,
    norm_gain,
    q_weight,
    kv_weight,
    out_weight,
    ctx_cache,
    span_start,
    finished_cache,
    block_dest,
):
    seq_count = lax.axis_size("seq")
    seq_place = lax.axis_index("seq")
    tok_rows = tokens.shape[0]
    kv_heads = kv_weight.shape[2] // HD
    head_group = q_weight.shape[1] // HD // kv_heads
    kv_width = kv_heads * HD
    ctx_rows = ctx_cache.reshape(ctx_cache.shape[0], 2 * kv_width)
    ctx_all = lax.all_gather(ctx_rows, "seq", axis=0, tiled=True)
    page_pool = move_pages(finished_cache, block_dest, seq_count, seq_place, kv_width)
    gathered = lax.all_gather(tokens, "tp", axis=1, tiled=True)
    widened = gathered.astype(jnp.float32)
    normed = (
        widened
        * lax.rsqrt(jnp.mean(widened * widened, axis=-1, keepdims=True) + rms_eps)
        * norm_gain
    ).astype(jnp.bfloat16)
    span_first = span_start[0]
    positions = (span_first + seq_place * tok_rows + jnp.arange(tok_rows, dtype=jnp.int32)).astype(
        jnp.float32
    )
    queries = jnp.dot(normed, q_weight, preferred_element_type=jnp.float32).reshape(
        tok_rows, kv_heads * head_group, HD
    )
    queries = rotate_pairs(queries, positions).astype(jnp.bfloat16)
    queries = jnp.transpose(queries, (1, 0, 2)).reshape(head_group * tok_rows, HD)
    projected = jnp.dot(
        normed, kv_weight.reshape(D, 2 * kv_width), preferred_element_type=jnp.float32
    ).reshape(tok_rows, 2, kv_heads, HD)
    new_keys = (
        rotate_pairs(projected[:, 0], positions).astype(jnp.bfloat16).reshape(tok_rows, kv_width)
    )
    new_values = projected[:, 1].astype(jnp.bfloat16).reshape(tok_rows, kv_width)
    new_rows = jnp.concatenate([new_keys, new_values], 1)
    arrived = [new_rows]
    for shift in range(1, seq_count):
        arrived.append(
            lax.ppermute(new_rows, "seq", [(s, s + shift) for s in range(seq_count - shift)])
        )
    new_all = jnp.concatenate(arrived, 0)
    query_rows = head_group * tok_rows
    scalars = jnp.stack([span_first, seq_place]).astype(jnp.int32)
    empty_state = (
        jnp.full((query_rows, 1), neg_fill, jnp.float32),
        jnp.zeros((query_rows, 1), jnp.float32),
        jnp.zeros((query_rows, HD), jnp.float32),
    )
    state = flash_pass(scalars, queries, ctx_all, empty_state, CTX_BLOCK, tok_rows, False)
    page_pool, state = lax.optimization_barrier((page_pool, state))
    row_max, row_total, summed = flash_pass(scalars, queries, new_all, state, CTX_BLOCK, tok_rows, True)
    mixed_heads = (
        (summed / row_total)
        .astype(jnp.bfloat16)
        .reshape(head_group, tok_rows, HD)
    )
    mixed_heads = jnp.transpose(mixed_heads, (1, 0, 2)).reshape(tok_rows, kv_width * head_group)
    tp_count = lax.axis_size("tp")
    tp_place = lax.axis_index("tp")
    out_cols = out_weight.shape[1] // tp_count
    partial = jnp.dot(mixed_heads, out_weight, preferred_element_type=jnp.float32)
    reduced = lax.dynamic_slice_in_dim(partial, tp_place * out_cols, out_cols, 1)
    partial = partial.astype(jnp.bfloat16)
    for shift in range(1, tp_count):
        chunk = lax.dynamic_slice_in_dim(
            partial, ((tp_place + shift) % tp_count) * out_cols, out_cols, 1
        )
        reduced = reduced + lax.ppermute(
            chunk, "tp", [(i, (i + shift) % tp_count) for i in range(tp_count)]
        ).astype(jnp.float32)
    attended = reduced.astype(jnp.bfloat16)
    return (attended, page_pool)


def solution(mesh):
    return jax.shard_map(
        on_device,
        mesh=mesh,
        in_specs=(
            P("seq", "tp"),
            P(),
            P(None, "tp"),
            P(None, None, "tp"),
            P("tp", None),
            P("seq", None, "tp"),
            P(),
            P(None, "seq", None, "tp"),
            P("seq", None),
        ),
        out_specs=(P("seq", "tp"), P(None, "seq", None, "tp")),
        check_vma=False,
    )
```

```python
import math
import functools

import jax
import jax.numpy as jnp
from jax import lax
from jax.experimental import pallas as pl
from jax.experimental.pallas import tpu as pltpu
from jax.sharding import PartitionSpec as P

D = 5120
HD = 128
LAYERS = 4
BLK = 16
CTX_BLOCK = 1024


rms_eps = 1e-06
rope_base = 1000000.0
neg_fill = -1e30


def rotate_pairs(values, positions):
    half_width = values.shape[-1] // 2
    frequency = jnp.exp(
        jnp.arange(half_width, dtype=jnp.float32) * (-2.0 * math.log(rope_base) / values.shape[-1])
    )
    angles = positions[:, None] * frequency[None, :]
    cosine = jnp.cos(angles)[:, None, :]
    sine_part = jnp.sin(angles)[:, None, :]
    first_half = values[..., :half_width]
    second_half = values[..., half_width:]
    return jnp.concatenate(
        [
            first_half * cosine - second_half * sine_part,
            second_half * cosine + first_half * sine_part,
        ],
        -1,
    )


def flash_kernel(
    scalars, q_ref, kv_ref, m_in, l_in, acc_in, m_ref, l_ref, acc_ref,
    *, block_rows, tok_rows, causal
):
    step = pl.program_id(0)
    span_first = scalars[0]
    seq_place = scalars[1]

    @pl.when(step == 0)
    def _():
        m_ref[...] = m_in[...]
        l_ref[...] = l_in[...]
        acc_ref[...] = acc_in[...]

    if causal:
        group = block_rows // tok_rows
        live = step * group <= seq_place
    else:
        key_first = step * block_rows
        live = key_first < span_first

    @pl.when(live)
    def _():
        q = q_ref[...]
        k = kv_ref[:, :HD]
        v = kv_ref[:, HD:]
        scores = lax.dot_general(
            q, k, (((1,), (1,)), ((), ())), preferred_element_type=jnp.float32
        ) * HD ** (-0.5)
        col = lax.broadcasted_iota(jnp.int32, scores.shape, 1)
        if causal:
            shift = tok_rows.bit_length() - 1
            distance = lax.shift_right_logical(col, shift) + step * group
            row = lax.broadcasted_iota(jnp.int32, scores.shape, 0) & (tok_rows - 1)
            visible = (distance <= seq_place) & (
                (distance > 0) | ((col & (tok_rows - 1)) <= row)
            )
        else:
            visible = col + key_first < span_first
        row_max = m_ref[...]
        new_max = jnp.maximum(row_max, jnp.max(jnp.where(visible, scores, neg_fill), 1, keepdims=True))
        weights = jnp.where(visible, jnp.exp(scores - new_max), 0.0)
        rescale = jnp.exp(row_max - new_max)
        l_ref[...] = l_ref[...] * rescale + jnp.sum(weights, 1, keepdims=True)
        acc_ref[...] = acc_ref[...] * rescale + jnp.dot(
            weights.astype(jnp.bfloat16), v, preferred_element_type=jnp.float32
        )
        m_ref[...] = new_max


def flash_pass(scalars, queries, kv_rows, state, block_rows, tok_rows, causal):
    rows = queries.shape[0]
    block_count = kv_rows.shape[0] // block_rows
    if causal:
        def kv_map(j, s):
            return (jnp.minimum(j, s[1] // (block_rows // tok_rows)), 0)
    else:
        def kv_map(j, s):
            last = (s[0] + block_rows - 1) // block_rows - 1
            return (jnp.maximum(jnp.minimum(j, last), 0), 0)
    full = lambda j, s: (0, 0)
    kernel = functools.partial(
        flash_kernel, block_rows=block_rows, tok_rows=tok_rows, causal=causal
    )
    return pl.pallas_call(
        kernel,
        out_shape=(
            jax.ShapeDtypeStruct((rows, 1), jnp.float32),
            jax.ShapeDtypeStruct((rows, 1), jnp.float32),
            jax.ShapeDtypeStruct((rows, HD), jnp.float32),
        ),
        grid_spec=pltpu.PrefetchScalarGridSpec(
            num_scalar_prefetch=1,
            grid=(block_count,),
            in_specs=[
                pl.BlockSpec((rows, HD), full),
                pl.BlockSpec((block_rows, 2 * HD), kv_map),
                pl.BlockSpec((rows, 1), full),
                pl.BlockSpec((rows, 1), full),
                pl.BlockSpec((rows, HD), full),
            ],
            out_specs=[
                pl.BlockSpec((rows, 1), full),
                pl.BlockSpec((rows, 1), full),
                pl.BlockSpec((rows, HD), full),
            ],
        ),
        compiler_params=pltpu.CompilerParams(
            dimension_semantics=("arbitrary",), vmem_limit_bytes=48 * 1024 * 1024
        ),
        cost_estimate=pl.CostEstimate(
            flops=4 * rows * HD * kv_rows.shape[0],
            transcendentals=rows * kv_rows.shape[0],
            bytes_accessed=kv_rows.size * 2 + rows * HD * 6,
        ),
    )(scalars, queries, kv_rows, *state)


def move_pages(finished_cache, block_dest, seq_count, seq_place, kv_width):
    block_total = block_dest.shape[0]
    capacity = 2 * block_total // seq_count
    destination = (block_dest[:, 0] - seq_place) % seq_count
    onehot = (destination[:, None] == jnp.arange(seq_count, dtype=jnp.int32)[None, :]).astype(
        jnp.int32
    )
    earlier_count = jnp.sum((jnp.cumsum(onehot, axis=0, dtype=jnp.int32) - onehot) * onehot, axis=1)
    slot_index = destination * capacity + earlier_count
    slot_match = slot_index[None, :] == jnp.arange(seq_count * capacity, dtype=jnp.int32)[:, None]
    filled = jnp.any(slot_match, axis=1)
    source_block = jnp.sum(
        jnp.where(slot_match, jnp.arange(block_total, dtype=jnp.int32)[None, :], 0), axis=1
    )
    blocks = finished_cache.reshape(LAYERS, block_total, BLK, 2, kv_width)
    outgoing = jnp.where(
        filled[None, :, None, None, None],
        jnp.take(blocks, source_block, axis=1),
        jnp.zeros((), blocks.dtype),
    )
    outgoing = outgoing.reshape(LAYERS, seq_count, capacity * BLK, 2, kv_width)
    piece_rows = capacity * BLK
    page_pool = jnp.zeros((LAYERS, seq_count * piece_rows, 2, kv_width), blocks.dtype)
    for shift in range(seq_count):
        piece = outgoing[:, shift]
        if shift:
            piece = lax.ppermute(
                piece, "seq", [(s, (s + shift) % seq_count) for s in range(seq_count)]
            )
        source = (seq_place - shift) % seq_count
        page_pool = lax.dynamic_update_slice(page_pool, piece, (0, source * piece_rows, 0, 0))
    return page_pool


def on_device(
    tokens,
    norm_gain,
    q_weight,
    kv_weight,
    out_weight,
    ctx_cache,
    span_start,
    finished_cache,
    block_dest,
):
    seq_count = lax.axis_size("seq")
    seq_place = lax.axis_index("seq")
    tok_rows = tokens.shape[0]
    kv_heads = kv_weight.shape[2] // HD
    head_group = q_weight.shape[1] // HD // kv_heads
    kv_width = kv_heads * HD
    ctx_rows = ctx_cache.reshape(ctx_cache.shape[0], 2 * kv_width)
    ctx_all = lax.all_gather(ctx_rows, "seq", axis=0, tiled=True)
    page_pool = move_pages(finished_cache, block_dest, seq_count, seq_place, kv_width)
    tp_count = lax.axis_size("tp")
    tp_place = lax.axis_index("tp")
    feature_cols = tokens.shape[1]
    gathered = jnp.zeros((tok_rows, feature_cols * tp_count), tokens.dtype)
    for shift in range(tp_count):
        piece = tokens
        if shift:
            piece = lax.ppermute(
                tokens, "tp", [(i, (i + shift) % tp_count) for i in range(tp_count)]
            )
        gathered = lax.dynamic_update_slice(
            gathered, piece, (0, ((tp_place - shift) % tp_count) * feature_cols)
        )
    widened = gathered.astype(jnp.float32)
    normed = (
        widened
        * lax.rsqrt(jnp.mean(widened * widened, axis=-1, keepdims=True) + rms_eps)
        * norm_gain
    ).astype(jnp.bfloat16)
    span_first = span_start[0]
    positions = (span_first + seq_place * tok_rows + jnp.arange(tok_rows, dtype=jnp.int32)).astype(
        jnp.float32
    )
    queries = jnp.dot(normed, q_weight, preferred_element_type=jnp.float32).reshape(
        tok_rows, kv_heads * head_group, HD
    )
    queries = rotate_pairs(queries, positions).astype(jnp.bfloat16)
    queries = jnp.transpose(queries, (1, 0, 2)).reshape(head_group * tok_rows, HD)
    projected = jnp.dot(
        normed, kv_weight.reshape(D, 2 * kv_width), preferred_element_type=jnp.float32
    ).reshape(tok_rows, 2, kv_heads, HD)
    new_keys = (
        rotate_pairs(projected[:, 0], positions).astype(jnp.bfloat16).reshape(tok_rows, kv_width)
    )
    new_values = projected[:, 1].astype(jnp.bfloat16).reshape(tok_rows, kv_width)
    new_rows = jnp.concatenate([new_keys, new_values], 1)
    arrived = [new_rows]
    for shift in range(1, seq_count):
        arrived.append(
            lax.ppermute(new_rows, "seq", [(s, s + shift) for s in range(seq_count - shift)])
        )
    new_all = jnp.concatenate(arrived, 0)
    query_rows = head_group * tok_rows
    scalars = jnp.stack([span_first, seq_place]).astype(jnp.int32)
    empty_state = (
        jnp.full((query_rows, 1), neg_fill, jnp.float32),
        jnp.zeros((query_rows, 1), jnp.float32),
        jnp.zeros((query_rows, HD), jnp.float32),
    )
    state = flash_pass(scalars, queries, ctx_all, empty_state, CTX_BLOCK, tok_rows, False)
    page_pool, state = lax.optimization_barrier((page_pool, state))
    row_max, row_total, summed = flash_pass(scalars, queries, new_all, state, CTX_BLOCK, tok_rows, True)
    mixed_heads = (
        (summed / row_total)
        .astype(jnp.bfloat16)
        .reshape(head_group, tok_rows, HD)
    )
    mixed_heads = jnp.transpose(mixed_heads, (1, 0, 2)).reshape(tok_rows, kv_width * head_group)
    out_cols = out_weight.shape[1] // tp_count
    partial = jnp.dot(mixed_heads, out_weight, preferred_element_type=jnp.float32)
    reduced = lax.dynamic_slice_in_dim(partial, tp_place * out_cols, out_cols, 1)
    partial = partial.astype(jnp.bfloat16)
    for shift in range(1, tp_count):
        chunk = lax.dynamic_slice_in_dim(
            partial, ((tp_place + shift) % tp_count) * out_cols, out_cols, 1
        )
        reduced = reduced + lax.ppermute(
            chunk, "tp", [(i, (i + shift) % tp_count) for i in range(tp_count)]
        ).astype(jnp.float32)
    attended = reduced.astype(jnp.bfloat16)
    return (attended, page_pool)


def solution(mesh):
    return jax.shard_map(
        on_device,
        mesh=mesh,
        in_specs=(
            P("seq", "tp"),
            P(),
            P(None, "tp"),
            P(None, None, "tp"),
            P("tp", None),
            P("seq", None, "tp"),
            P(),
            P(None, "seq", None, "tp"),
            P("seq", None),
        ),
        out_specs=(P("seq", "tp"), P(None, "seq", None, "tp")),
        check_vma=False,
    )
```

```python
import math
import functools

import jax
import jax.numpy as jnp
from jax import lax
from jax.experimental import pallas as pl
from jax.experimental.pallas import tpu as pltpu
from jax.sharding import PartitionSpec as P

D = 5120
HD = 128
LAYERS = 4
BLK = 16
CTX_BLOCK = 1024


rms_eps = 1e-06
rope_base = 1000000.0
neg_fill = -1e30


def rotate_pairs(values, positions):
    half_width = values.shape[-1] // 2
    frequency = jnp.exp(
        jnp.arange(half_width, dtype=jnp.float32) * (-2.0 * math.log(rope_base) / values.shape[-1])
    )
    angles = positions[:, None] * frequency[None, :]
    cosine = jnp.cos(angles)[:, None, :]
    sine_part = jnp.sin(angles)[:, None, :]
    first_half = values[..., :half_width]
    second_half = values[..., half_width:]
    return jnp.concatenate(
        [
            first_half * cosine - second_half * sine_part,
            second_half * cosine + first_half * sine_part,
        ],
        -1,
    )


def flash_kernel(
    scalars, q_ref, kv_ref, m_in, l_in, acc_in, m_ref, l_ref, acc_ref,
    *, block_rows, tok_rows, causal
):
    step = pl.program_id(0)
    span_first = scalars[0]
    seq_place = scalars[1]

    @pl.when(step == 0)
    def _():
        m_ref[...] = m_in[...]
        l_ref[...] = l_in[...]
        acc_ref[...] = acc_in[...]

    if causal:
        group = block_rows // tok_rows
        live = step * group <= seq_place
    else:
        key_first = step * block_rows
        live = key_first < span_first

    @pl.when(live)
    def _():
        q = q_ref[...]
        k = kv_ref[:, :HD]
        v = kv_ref[:, HD:]
        scores = lax.dot_general(
            q, k, (((1,), (1,)), ((), ())), preferred_element_type=jnp.float32
        ) * HD ** (-0.5)
        col = lax.broadcasted_iota(jnp.int32, scores.shape, 1)
        if causal:
            shift = tok_rows.bit_length() - 1
            distance = lax.shift_right_logical(col, shift) + step * group
            row = lax.broadcasted_iota(jnp.int32, scores.shape, 0) & (tok_rows - 1)
            visible = (distance <= seq_place) & (
                (distance > 0) | ((col & (tok_rows - 1)) <= row)
            )
        else:
            visible = col + key_first < span_first
        row_max = m_ref[...]
        new_max = jnp.maximum(row_max, jnp.max(jnp.where(visible, scores, neg_fill), 1, keepdims=True))
        weights = jnp.where(visible, jnp.exp(scores - new_max), 0.0)
        rescale = jnp.exp(row_max - new_max)
        l_ref[...] = l_ref[...] * rescale + jnp.sum(weights, 1, keepdims=True)
        acc_ref[...] = acc_ref[...] * rescale + jnp.dot(
            weights.astype(jnp.bfloat16), v, preferred_element_type=jnp.float32
        )
        m_ref[...] = new_max


def flash_pass(scalars, queries, kv_rows, state, block_rows, tok_rows, causal):
    rows = queries.shape[0]
    block_count = kv_rows.shape[0] // block_rows
    if causal:
        def kv_map(j, s):
            return (jnp.minimum(j, s[1] // (block_rows // tok_rows)), 0)
    else:
        def kv_map(j, s):
            last = (s[0] + block_rows - 1) // block_rows - 1
            return (jnp.maximum(jnp.minimum(j, last), 0), 0)
    full = lambda j, s: (0, 0)
    kernel = functools.partial(
        flash_kernel, block_rows=block_rows, tok_rows=tok_rows, causal=causal
    )
    return pl.pallas_call(
        kernel,
        out_shape=(
            jax.ShapeDtypeStruct((rows, 1), jnp.float32),
            jax.ShapeDtypeStruct((rows, 1), jnp.float32),
            jax.ShapeDtypeStruct((rows, HD), jnp.float32),
        ),
        grid_spec=pltpu.PrefetchScalarGridSpec(
            num_scalar_prefetch=1,
            grid=(block_count,),
            in_specs=[
                pl.BlockSpec((rows, HD), full),
                pl.BlockSpec((block_rows, 2 * HD), kv_map),
                pl.BlockSpec((rows, 1), full),
                pl.BlockSpec((rows, 1), full),
                pl.BlockSpec((rows, HD), full),
            ],
            out_specs=[
                pl.BlockSpec((rows, 1), full),
                pl.BlockSpec((rows, 1), full),
                pl.BlockSpec((rows, HD), full),
            ],
        ),
        compiler_params=pltpu.CompilerParams(
            dimension_semantics=("arbitrary",), vmem_limit_bytes=48 * 1024 * 1024
        ),
        cost_estimate=pl.CostEstimate(
            flops=4 * rows * HD * kv_rows.shape[0],
            transcendentals=rows * kv_rows.shape[0],
            bytes_accessed=kv_rows.size * 2 + rows * HD * 6,
        ),
    )(scalars, queries, kv_rows, *state)


def move_pages(finished_cache, block_dest, seq_count, seq_place, kv_width):
    block_total = block_dest.shape[0]
    capacity = 2 * block_total // seq_count
    destination = (block_dest[:, 0] - seq_place) % seq_count
    onehot = (destination[:, None] == jnp.arange(seq_count, dtype=jnp.int32)[None, :]).astype(
        jnp.int32
    )
    earlier_count = jnp.sum((jnp.cumsum(onehot, axis=0, dtype=jnp.int32) - onehot) * onehot, axis=1)
    slot_index = destination * capacity + earlier_count
    slot_match = slot_index[None, :] == jnp.arange(seq_count * capacity, dtype=jnp.int32)[:, None]
    filled = jnp.any(slot_match, axis=1)
    source_block = jnp.sum(
        jnp.where(slot_match, jnp.arange(block_total, dtype=jnp.int32)[None, :], 0), axis=1
    )
    blocks = finished_cache.reshape(LAYERS, block_total, BLK, 2, kv_width)
    outgoing = jnp.where(
        filled[None, :, None, None, None],
        jnp.take(blocks, source_block, axis=1),
        jnp.zeros((), blocks.dtype),
    )
    outgoing = outgoing.reshape(LAYERS, seq_count, capacity * BLK, 2, kv_width)
    piece_rows = capacity * BLK
    page_pool = jnp.zeros((LAYERS, seq_count * piece_rows, 2, kv_width), blocks.dtype)
    for shift in range(seq_count):
        piece = outgoing[:, shift]
        if shift:
            piece = lax.ppermute(
                piece, "seq", [(s, (s + shift) % seq_count) for s in range(seq_count)]
            )
        source = (seq_place - shift) % seq_count
        page_pool = lax.dynamic_update_slice(page_pool, piece, (0, source * piece_rows, 0, 0))
    return page_pool


def on_device(
    tokens,
    norm_gain,
    q_weight,
    kv_weight,
    out_weight,
    ctx_cache,
    span_start,
    finished_cache,
    block_dest,
):
    seq_count = lax.axis_size("seq")
    seq_place = lax.axis_index("seq")
    tok_rows = tokens.shape[0]
    kv_heads = kv_weight.shape[2] // HD
    head_group = q_weight.shape[1] // HD // kv_heads
    kv_width = kv_heads * HD
    ctx_rows = ctx_cache.reshape(ctx_cache.shape[0], 2 * kv_width)
    ctx_all = lax.all_gather(ctx_rows, "seq", axis=0, tiled=True)
    page_pool = move_pages(finished_cache, block_dest, seq_count, seq_place, kv_width)
    gathered = lax.all_gather(tokens, "tp", axis=1, tiled=True)
    widened = gathered.astype(jnp.float32)
    normed = (
        widened
        * lax.rsqrt(jnp.mean(widened * widened, axis=-1, keepdims=True) + rms_eps)
        * norm_gain
    ).astype(jnp.bfloat16)
    span_first = span_start[0]
    positions = (span_first + seq_place * tok_rows + jnp.arange(tok_rows, dtype=jnp.int32)).astype(
        jnp.float32
    )
    queries = jnp.dot(normed, q_weight, preferred_element_type=jnp.float32).reshape(
        tok_rows, kv_heads * head_group, HD
    )
    queries = rotate_pairs(queries, positions).astype(jnp.bfloat16)
    queries = jnp.transpose(queries, (1, 0, 2)).reshape(head_group * tok_rows, HD)
    projected = jnp.dot(
        normed, kv_weight.reshape(D, 2 * kv_width), preferred_element_type=jnp.float32
    ).reshape(tok_rows, 2, kv_heads, HD)
    new_keys = (
        rotate_pairs(projected[:, 0], positions).astype(jnp.bfloat16).reshape(tok_rows, kv_width)
    )
    new_values = projected[:, 1].astype(jnp.bfloat16).reshape(tok_rows, kv_width)
    new_rows = jnp.concatenate([new_keys, new_values], 1)
    arrived = [new_rows]
    for shift in range(1, seq_count):
        arrived.append(
            lax.ppermute(new_rows, "seq", [(s, s + shift) for s in range(seq_count - shift)])
        )
    new_all = jnp.concatenate(arrived, 0)
    query_rows = head_group * tok_rows
    scalars = jnp.stack([span_first, seq_place]).astype(jnp.int32)
    empty_state = (
        jnp.full((query_rows, 1), neg_fill, jnp.float32),
        jnp.zeros((query_rows, 1), jnp.float32),
        jnp.zeros((query_rows, HD), jnp.float32),
    )
    state = flash_pass(scalars, queries, ctx_all, empty_state, CTX_BLOCK, tok_rows, False)
    page_pool, state = lax.optimization_barrier((page_pool, state))
    row_max, row_total, summed = flash_pass(scalars, queries, new_all, state, CTX_BLOCK, tok_rows, True)
    mixed_heads = (
        (summed / row_total)
        .astype(jnp.bfloat16)
        .reshape(head_group, tok_rows, HD)
    )
    mixed_heads = jnp.transpose(mixed_heads, (1, 0, 2)).reshape(tok_rows, kv_width * head_group)
    tp_count = lax.axis_size("tp")
    tp_place = lax.axis_index("tp")
    out_cols = out_weight.shape[1] // tp_count
    partial = jnp.dot(mixed_heads, out_weight, preferred_element_type=jnp.float32)
    ring = 4
    pairs = tp_count // ring
    pair_place = tp_place // ring
    ring_place = tp_place % ring
    half_cols = ring * out_cols
    kept = lax.dynamic_slice_in_dim(partial, pair_place * half_cols, half_cols, 1)
    for step in range(1, pairs):
        other = (pair_place + step) % pairs
        sent = lax.dynamic_slice_in_dim(partial, other * half_cols, half_cols, 1)
        kept = kept + lax.ppermute(
            sent.astype(jnp.bfloat16),
            "tp",
            [(i, ((i // ring + step) % pairs) * ring + i % ring) for i in range(tp_count)],
        ).astype(jnp.float32)
    reduced = lax.dynamic_slice_in_dim(kept, ring_place * out_cols, out_cols, 1)
    kept = kept.astype(jnp.bfloat16)
    for shift in range(1, ring):
        chunk = lax.dynamic_slice_in_dim(kept, ((ring_place + shift) % ring) * out_cols, out_cols, 1)
        reduced = reduced + lax.ppermute(
            chunk,
            "tp",
            [(i, (i // ring) * ring + (i % ring + shift) % ring) for i in range(tp_count)],
        ).astype(jnp.float32)
    attended = reduced.astype(jnp.bfloat16)
    return (attended, page_pool)


def solution(mesh):
    return jax.shard_map(
        on_device,
        mesh=mesh,
        in_specs=(
            P("seq", "tp"),
            P(),
            P(None, "tp"),
            P(None, None, "tp"),
            P("tp", None),
            P("seq", None, "tp"),
            P(),
            P(None, "seq", None, "tp"),
            P("seq", None),
        ),
        out_specs=(P("seq", "tp"), P(None, "seq", None, "tp")),
        check_vma=False,
    )
```

```python
import math
import functools

import jax
import jax.numpy as jnp
from jax import lax
from jax.experimental import pallas as pl
from jax.experimental.pallas import tpu as pltpu
from jax.sharding import PartitionSpec as P

D = 5120
HD = 128
LAYERS = 4
BLK = 16
CTX_BLOCK = 1024


rms_eps = 1e-06
rope_base = 1000000.0
neg_fill = -1e30


def rotate_pairs(values, positions):
    half_width = values.shape[-1] // 2
    frequency = jnp.exp(
        jnp.arange(half_width, dtype=jnp.float32) * (-2.0 * math.log(rope_base) / values.shape[-1])
    )
    angles = positions[:, None] * frequency[None, :]
    cosine = jnp.cos(angles)[:, None, :]
    sine_part = jnp.sin(angles)[:, None, :]
    first_half = values[..., :half_width]
    second_half = values[..., half_width:]
    return jnp.concatenate(
        [
            first_half * cosine - second_half * sine_part,
            second_half * cosine + first_half * sine_part,
        ],
        -1,
    )


def flash_kernel(
    scalars, q_ref, kv_ref, m_in, l_in, acc_in, m_ref, l_ref, acc_ref,
    *, block_rows, tok_rows, causal
):
    step = pl.program_id(0)
    span_first = scalars[0]
    seq_place = scalars[1]

    @pl.when(step == 0)
    def _():
        m_ref[...] = m_in[...]
        l_ref[...] = l_in[...]
        acc_ref[...] = acc_in[...]

    if causal:
        group = block_rows // tok_rows
        live = step * group <= seq_place
    else:
        key_first = step * block_rows
        live = key_first < span_first

    @pl.when(live)
    def _():
        q = q_ref[...]
        k = kv_ref[:, :HD]
        v = kv_ref[:, HD:]
        scores = lax.dot_general(
            q, k, (((1,), (1,)), ((), ())), preferred_element_type=jnp.float32
        ) * HD ** (-0.5)
        col = lax.broadcasted_iota(jnp.int32, scores.shape, 1)
        if causal:
            shift = tok_rows.bit_length() - 1
            distance = lax.shift_right_logical(col, shift) + step * group
            row = lax.broadcasted_iota(jnp.int32, scores.shape, 0) & (tok_rows - 1)
            visible = (distance <= seq_place) & (
                (distance > 0) | ((col & (tok_rows - 1)) <= row)
            )
        else:
            visible = col + key_first < span_first
        row_max = m_ref[...]
        new_max = jnp.maximum(row_max, jnp.max(jnp.where(visible, scores, neg_fill), 1, keepdims=True))
        weights = jnp.exp(jnp.where(visible, scores, neg_fill) - new_max)
        rescale = jnp.exp(row_max - new_max)
        l_ref[...] = l_ref[...] * rescale + jnp.sum(weights, 1, keepdims=True)
        acc_ref[...] = acc_ref[...] * rescale + jnp.dot(
            weights.astype(jnp.bfloat16), v, preferred_element_type=jnp.float32
        )
        m_ref[...] = new_max


def flash_pass(scalars, queries, kv_rows, state, block_rows, tok_rows, causal):
    rows = queries.shape[0]
    block_count = kv_rows.shape[0] // block_rows
    if causal:
        def kv_map(j, s):
            return (jnp.minimum(j, s[1] // (block_rows // tok_rows)), 0)
    else:
        def kv_map(j, s):
            last = (s[0] + block_rows - 1) // block_rows - 1
            return (jnp.maximum(jnp.minimum(j, last), 0), 0)
    full = lambda j, s: (0, 0)
    kernel = functools.partial(
        flash_kernel, block_rows=block_rows, tok_rows=tok_rows, causal=causal
    )
    return pl.pallas_call(
        kernel,
        out_shape=(
            jax.ShapeDtypeStruct((rows, 1), jnp.float32),
            jax.ShapeDtypeStruct((rows, 1), jnp.float32),
            jax.ShapeDtypeStruct((rows, HD), jnp.float32),
        ),
        grid_spec=pltpu.PrefetchScalarGridSpec(
            num_scalar_prefetch=1,
            grid=(block_count,),
            in_specs=[
                pl.BlockSpec((rows, HD), full),
                pl.BlockSpec((block_rows, 2 * HD), kv_map),
                pl.BlockSpec((rows, 1), full),
                pl.BlockSpec((rows, 1), full),
                pl.BlockSpec((rows, HD), full),
            ],
            out_specs=[
                pl.BlockSpec((rows, 1), full),
                pl.BlockSpec((rows, 1), full),
                pl.BlockSpec((rows, HD), full),
            ],
        ),
        compiler_params=pltpu.CompilerParams(
            dimension_semantics=("arbitrary",), vmem_limit_bytes=48 * 1024 * 1024
        ),
        cost_estimate=pl.CostEstimate(
            flops=4 * rows * HD * kv_rows.shape[0],
            transcendentals=rows * kv_rows.shape[0],
            bytes_accessed=kv_rows.size * 2 + rows * HD * 6,
        ),
    )(scalars, queries, kv_rows, *state)


def move_pages(finished_cache, block_dest, seq_count, seq_place, kv_width):
    block_total = block_dest.shape[0]
    capacity = 2 * block_total // seq_count
    destination = (block_dest[:, 0] - seq_place) % seq_count
    onehot = (destination[:, None] == jnp.arange(seq_count, dtype=jnp.int32)[None, :]).astype(
        jnp.int32
    )
    earlier_count = jnp.sum((jnp.cumsum(onehot, axis=0, dtype=jnp.int32) - onehot) * onehot, axis=1)
    slot_index = destination * capacity + earlier_count
    slot_match = slot_index[None, :] == jnp.arange(seq_count * capacity, dtype=jnp.int32)[:, None]
    filled = jnp.any(slot_match, axis=1)
    source_block = jnp.sum(
        jnp.where(slot_match, jnp.arange(block_total, dtype=jnp.int32)[None, :], 0), axis=1
    )
    blocks = finished_cache.reshape(LAYERS, block_total, BLK, 2, kv_width)
    outgoing = jnp.where(
        filled[None, :, None, None, None],
        jnp.take(blocks, source_block, axis=1),
        jnp.zeros((), blocks.dtype),
    )
    outgoing = outgoing.reshape(LAYERS, seq_count, capacity * BLK, 2, kv_width)
    piece_rows = capacity * BLK
    page_pool = jnp.zeros((LAYERS, seq_count * piece_rows, 2, kv_width), blocks.dtype)
    for shift in range(seq_count):
        piece = outgoing[:, shift]
        if shift:
            piece = lax.ppermute(
                piece, "seq", [(s, (s + shift) % seq_count) for s in range(seq_count)]
            )
        source = (seq_place - shift) % seq_count
        page_pool = lax.dynamic_update_slice(page_pool, piece, (0, source * piece_rows, 0, 0))
    return page_pool


def on_device(
    tokens,
    norm_gain,
    q_weight,
    kv_weight,
    out_weight,
    ctx_cache,
    span_start,
    finished_cache,
    block_dest,
):
    seq_count = lax.axis_size("seq")
    seq_place = lax.axis_index("seq")
    tok_rows = tokens.shape[0]
    kv_heads = kv_weight.shape[2] // HD
    head_group = q_weight.shape[1] // HD // kv_heads
    kv_width = kv_heads * HD
    ctx_rows = ctx_cache.reshape(ctx_cache.shape[0], 2 * kv_width)
    ctx_all = lax.all_gather(ctx_rows, "seq", axis=0, tiled=True)
    page_pool = move_pages(finished_cache, block_dest, seq_count, seq_place, kv_width)
    gathered = lax.all_gather(tokens, "tp", axis=1, tiled=True)
    widened = gathered.astype(jnp.float32)
    normed = (
        widened
        * lax.rsqrt(jnp.mean(widened * widened, axis=-1, keepdims=True) + rms_eps)
        * norm_gain
    ).astype(jnp.bfloat16)
    span_first = span_start[0]
    positions = (span_first + seq_place * tok_rows + jnp.arange(tok_rows, dtype=jnp.int32)).astype(
        jnp.float32
    )
    queries = jnp.dot(normed, q_weight, preferred_element_type=jnp.float32).reshape(
        tok_rows, kv_heads * head_group, HD
    )
    queries = rotate_pairs(queries, positions).astype(jnp.bfloat16)
    queries = jnp.transpose(queries, (1, 0, 2)).reshape(head_group * tok_rows, HD)
    projected = jnp.dot(
        normed, kv_weight.reshape(D, 2 * kv_width), preferred_element_type=jnp.float32
    ).reshape(tok_rows, 2, kv_heads, HD)
    new_keys = (
        rotate_pairs(projected[:, 0], positions).astype(jnp.bfloat16).reshape(tok_rows, kv_width)
    )
    new_values = projected[:, 1].astype(jnp.bfloat16).reshape(tok_rows, kv_width)
    new_rows = jnp.concatenate([new_keys, new_values], 1)
    arrived = [new_rows]
    for shift in range(1, seq_count):
        arrived.append(
            lax.ppermute(new_rows, "seq", [(s, s + shift) for s in range(seq_count - shift)])
        )
    new_all = jnp.concatenate(arrived, 0)
    query_rows = head_group * tok_rows
    scalars = jnp.stack([span_first, seq_place]).astype(jnp.int32)
    empty_state = (
        jnp.full((query_rows, 1), neg_fill, jnp.float32),
        jnp.zeros((query_rows, 1), jnp.float32),
        jnp.zeros((query_rows, HD), jnp.float32),
    )
    state = flash_pass(scalars, queries, ctx_all, empty_state, CTX_BLOCK, tok_rows, False)
    page_pool, state = lax.optimization_barrier((page_pool, state))
    row_max, row_total, summed = flash_pass(scalars, queries, new_all, state, CTX_BLOCK, tok_rows, True)
    mixed_heads = (
        (summed / row_total)
        .astype(jnp.bfloat16)
        .reshape(head_group, tok_rows, HD)
    )
    mixed_heads = jnp.transpose(mixed_heads, (1, 0, 2)).reshape(tok_rows, kv_width * head_group)
    tp_count = lax.axis_size("tp")
    tp_place = lax.axis_index("tp")
    out_cols = out_weight.shape[1] // tp_count
    partial = jnp.dot(mixed_heads, out_weight, preferred_element_type=jnp.float32)
    reduced = lax.dynamic_slice_in_dim(partial, tp_place * out_cols, out_cols, 1)
    partial = partial.astype(jnp.bfloat16)
    for shift in range(1, tp_count):
        chunk = lax.dynamic_slice_in_dim(
            partial, ((tp_place + shift) % tp_count) * out_cols, out_cols, 1
        )
        reduced = reduced + lax.ppermute(
            chunk, "tp", [(i, (i + shift) % tp_count) for i in range(tp_count)]
        ).astype(jnp.float32)
    attended = reduced.astype(jnp.bfloat16)
    return (attended, page_pool)


def solution(mesh):
    return jax.shard_map(
        on_device,
        mesh=mesh,
        in_specs=(
            P("seq", "tp"),
            P(),
            P(None, "tp"),
            P(None, None, "tp"),
            P("tp", None),
            P("seq", None, "tp"),
            P(),
            P(None, "seq", None, "tp"),
            P("seq", None),
        ),
        out_specs=(P("seq", "tp"), P(None, "seq", None, "tp")),
        check_vma=False,
    )
```

```python
import math
import functools

import jax
import jax.numpy as jnp
from jax import lax
from jax.experimental import pallas as pl
from jax.experimental.pallas import tpu as pltpu
from jax.sharding import PartitionSpec as P

D = 5120
HD = 128
LAYERS = 4
BLK = 16
CTX_BLOCK = 2048
NEW_BLOCK = 1024


rms_eps = 1e-06
rope_base = 1000000.0
neg_fill = -1e30


def rotate_pairs(values, positions):
    half_width = values.shape[-1] // 2
    frequency = jnp.exp(
        jnp.arange(half_width, dtype=jnp.float32) * (-2.0 * math.log(rope_base) / values.shape[-1])
    )
    angles = positions[:, None] * frequency[None, :]
    cosine = jnp.cos(angles)[:, None, :]
    sine_part = jnp.sin(angles)[:, None, :]
    first_half = values[..., :half_width]
    second_half = values[..., half_width:]
    return jnp.concatenate(
        [
            first_half * cosine - second_half * sine_part,
            second_half * cosine + first_half * sine_part,
        ],
        -1,
    )


def flash_kernel(
    scalars, q_ref, kv_ref, m_in, l_in, acc_in, m_ref, l_ref, acc_ref,
    *, block_rows, tok_rows, causal
):
    step = pl.program_id(0)
    span_first = scalars[0]
    seq_place = scalars[1]

    @pl.when(step == 0)
    def _():
        m_ref[...] = m_in[...]
        l_ref[...] = l_in[...]
        acc_ref[...] = acc_in[...]

    if causal:
        group = block_rows // tok_rows
        live = step * group <= seq_place
    else:
        key_first = step * block_rows
        live = key_first < span_first

    @pl.when(live)
    def _():
        q = q_ref[...]
        k = kv_ref[:, :HD]
        v = kv_ref[:, HD:]
        scores = lax.dot_general(
            q, k, (((1,), (1,)), ((), ())), preferred_element_type=jnp.float32
        ) * HD ** (-0.5)
        col = lax.broadcasted_iota(jnp.int32, scores.shape, 1)
        if causal:
            shift = tok_rows.bit_length() - 1
            distance = lax.shift_right_logical(col, shift) + step * group
            row = lax.broadcasted_iota(jnp.int32, scores.shape, 0) & (tok_rows - 1)
            visible = (distance <= seq_place) & (
                (distance > 0) | ((col & (tok_rows - 1)) <= row)
            )
        else:
            visible = col + key_first < span_first
        row_max = m_ref[...]
        new_max = jnp.maximum(row_max, jnp.max(jnp.where(visible, scores, neg_fill), 1, keepdims=True))
        weights = jnp.exp(jnp.where(visible, scores, neg_fill) - new_max)
        rescale = jnp.exp(row_max - new_max)
        l_ref[...] = l_ref[...] * rescale + jnp.sum(weights, 1, keepdims=True)
        acc_ref[...] = acc_ref[...] * rescale + jnp.dot(
            weights.astype(jnp.bfloat16), v, preferred_element_type=jnp.float32
        )
        m_ref[...] = new_max


def flash_pass(scalars, queries, kv_rows, state, block_rows, tok_rows, causal):
    rows = queries.shape[0]
    block_count = kv_rows.shape[0] // block_rows
    if causal:
        def kv_map(j, s):
            return (jnp.minimum(j, s[1] // (block_rows // tok_rows)), 0)
    else:
        def kv_map(j, s):
            last = (s[0] + block_rows - 1) // block_rows - 1
            return (jnp.maximum(jnp.minimum(j, last), 0), 0)
    full = lambda j, s: (0, 0)
    kernel = functools.partial(
        flash_kernel, block_rows=block_rows, tok_rows=tok_rows, causal=causal
    )
    return pl.pallas_call(
        kernel,
        out_shape=(
            jax.ShapeDtypeStruct((rows, 1), jnp.float32),
            jax.ShapeDtypeStruct((rows, 1), jnp.float32),
            jax.ShapeDtypeStruct((rows, HD), jnp.float32),
        ),
        grid_spec=pltpu.PrefetchScalarGridSpec(
            num_scalar_prefetch=1,
            grid=(block_count,),
            in_specs=[
                pl.BlockSpec((rows, HD), full),
                pl.BlockSpec((block_rows, 2 * HD), kv_map),
                pl.BlockSpec((rows, 1), full),
                pl.BlockSpec((rows, 1), full),
                pl.BlockSpec((rows, HD), full),
            ],
            out_specs=[
                pl.BlockSpec((rows, 1), full),
                pl.BlockSpec((rows, 1), full),
                pl.BlockSpec((rows, HD), full),
            ],
        ),
        compiler_params=pltpu.CompilerParams(
            dimension_semantics=("arbitrary",), vmem_limit_bytes=48 * 1024 * 1024
        ),
        cost_estimate=pl.CostEstimate(
            flops=4 * rows * HD * kv_rows.shape[0],
            transcendentals=rows * kv_rows.shape[0],
            bytes_accessed=kv_rows.size * 2 + rows * HD * 6,
        ),
    )(scalars, queries, kv_rows, *state)


def move_pages(finished_cache, block_dest, seq_count, seq_place, kv_width):
    block_total = block_dest.shape[0]
    capacity = 2 * block_total // seq_count
    destination = (block_dest[:, 0] - seq_place) % seq_count
    onehot = (destination[:, None] == jnp.arange(seq_count, dtype=jnp.int32)[None, :]).astype(
        jnp.int32
    )
    earlier_count = jnp.sum((jnp.cumsum(onehot, axis=0, dtype=jnp.int32) - onehot) * onehot, axis=1)
    slot_index = destination * capacity + earlier_count
    slot_match = slot_index[None, :] == jnp.arange(seq_count * capacity, dtype=jnp.int32)[:, None]
    filled = jnp.any(slot_match, axis=1)
    source_block = jnp.sum(
        jnp.where(slot_match, jnp.arange(block_total, dtype=jnp.int32)[None, :], 0), axis=1
    )
    blocks = finished_cache.reshape(LAYERS, block_total, BLK, 2, kv_width)
    outgoing = jnp.where(
        filled[None, :, None, None, None],
        jnp.take(blocks, source_block, axis=1),
        jnp.zeros((), blocks.dtype),
    )
    outgoing = outgoing.reshape(LAYERS, seq_count, capacity * BLK, 2, kv_width)
    piece_rows = capacity * BLK
    page_pool = jnp.zeros((LAYERS, seq_count * piece_rows, 2, kv_width), blocks.dtype)
    for shift in range(seq_count):
        piece = outgoing[:, shift]
        if shift:
            piece = lax.ppermute(
                piece, "seq", [(s, (s + shift) % seq_count) for s in range(seq_count)]
            )
        source = (seq_place - shift) % seq_count
        page_pool = lax.dynamic_update_slice(page_pool, piece, (0, source * piece_rows, 0, 0))
    return page_pool


def on_device(
    tokens,
    norm_gain,
    q_weight,
    kv_weight,
    out_weight,
    ctx_cache,
    span_start,
    finished_cache,
    block_dest,
):
    seq_count = lax.axis_size("seq")
    seq_place = lax.axis_index("seq")
    tok_rows = tokens.shape[0]
    kv_heads = kv_weight.shape[2] // HD
    head_group = q_weight.shape[1] // HD // kv_heads
    kv_width = kv_heads * HD
    ctx_rows = ctx_cache.reshape(ctx_cache.shape[0], 2 * kv_width)
    ctx_all = lax.all_gather(ctx_rows, "seq", axis=0, tiled=True)
    page_pool = move_pages(finished_cache, block_dest, seq_count, seq_place, kv_width)
    gathered = lax.all_gather(tokens, "tp", axis=1, tiled=True)
    widened = gathered.astype(jnp.float32)
    normed = (
        widened
        * lax.rsqrt(jnp.mean(widened * widened, axis=-1, keepdims=True) + rms_eps)
        * norm_gain
    ).astype(jnp.bfloat16)
    span_first = span_start[0]
    positions = (span_first + seq_place * tok_rows + jnp.arange(tok_rows, dtype=jnp.int32)).astype(
        jnp.float32
    )
    queries = jnp.dot(normed, q_weight, preferred_element_type=jnp.float32).reshape(
        tok_rows, kv_heads * head_group, HD
    )
    queries = rotate_pairs(queries, positions).astype(jnp.bfloat16)
    queries = jnp.transpose(queries, (1, 0, 2)).reshape(head_group * tok_rows, HD)
    projected = jnp.dot(
        normed, kv_weight.reshape(D, 2 * kv_width), preferred_element_type=jnp.float32
    ).reshape(tok_rows, 2, kv_heads, HD)
    new_keys = (
        rotate_pairs(projected[:, 0], positions).astype(jnp.bfloat16).reshape(tok_rows, kv_width)
    )
    new_values = projected[:, 1].astype(jnp.bfloat16).reshape(tok_rows, kv_width)
    new_rows = jnp.concatenate([new_keys, new_values], 1)
    arrived = [new_rows]
    for shift in range(1, seq_count):
        arrived.append(
            lax.ppermute(new_rows, "seq", [(s, s + shift) for s in range(seq_count - shift)])
        )
    new_all = jnp.concatenate(arrived, 0)
    query_rows = head_group * tok_rows
    scalars = jnp.stack([span_first, seq_place]).astype(jnp.int32)
    empty_state = (
        jnp.full((query_rows, 1), neg_fill, jnp.float32),
        jnp.zeros((query_rows, 1), jnp.float32),
        jnp.zeros((query_rows, HD), jnp.float32),
    )
    state = flash_pass(scalars, queries, ctx_all, empty_state, CTX_BLOCK, tok_rows, False)
    page_pool, state = lax.optimization_barrier((page_pool, state))
    row_max, row_total, summed = flash_pass(scalars, queries, new_all, state, NEW_BLOCK, tok_rows, True)
    mixed_heads = (
        (summed / row_total)
        .astype(jnp.bfloat16)
        .reshape(head_group, tok_rows, HD)
    )
    mixed_heads = jnp.transpose(mixed_heads, (1, 0, 2)).reshape(tok_rows, kv_width * head_group)
    tp_count = lax.axis_size("tp")
    tp_place = lax.axis_index("tp")
    out_cols = out_weight.shape[1] // tp_count
    partial = jnp.dot(mixed_heads, out_weight, preferred_element_type=jnp.float32)
    reduced = lax.dynamic_slice_in_dim(partial, tp_place * out_cols, out_cols, 1)
    partial = partial.astype(jnp.bfloat16)
    for shift in range(1, tp_count):
        chunk = lax.dynamic_slice_in_dim(
            partial, ((tp_place + shift) % tp_count) * out_cols, out_cols, 1
        )
        reduced = reduced + lax.ppermute(
            chunk, "tp", [(i, (i + shift) % tp_count) for i in range(tp_count)]
        ).astype(jnp.float32)
    attended = reduced.astype(jnp.bfloat16)
    return (attended, page_pool)


def solution(mesh):
    return jax.shard_map(
        on_device,
        mesh=mesh,
        in_specs=(
            P("seq", "tp"),
            P(),
            P(None, "tp"),
            P(None, None, "tp"),
            P("tp", None),
            P("seq", None, "tp"),
            P(),
            P(None, "seq", None, "tp"),
            P("seq", None),
        ),
        out_specs=(P("seq", "tp"), P(None, "seq", None, "tp")),
        check_vma=False,
    )
```

```python
import math
import functools

import jax
import jax.numpy as jnp
from jax import lax
from jax.experimental import pallas as pl
from jax.experimental.pallas import tpu as pltpu
from jax.sharding import PartitionSpec as P

D = 5120
HD = 128
LAYERS = 4
BLK = 16
CTX_BLOCK = 512
NEW_BLOCK = 1024


rms_eps = 1e-06
rope_base = 1000000.0
neg_fill = -1e30


def rotate_pairs(values, positions):
    half_width = values.shape[-1] // 2
    frequency = jnp.exp(
        jnp.arange(half_width, dtype=jnp.float32) * (-2.0 * math.log(rope_base) / values.shape[-1])
    )
    angles = positions[:, None] * frequency[None, :]
    cosine = jnp.cos(angles)[:, None, :]
    sine_part = jnp.sin(angles)[:, None, :]
    first_half = values[..., :half_width]
    second_half = values[..., half_width:]
    return jnp.concatenate(
        [
            first_half * cosine - second_half * sine_part,
            second_half * cosine + first_half * sine_part,
        ],
        -1,
    )


def flash_kernel(
    scalars, q_ref, kv_ref, m_in, l_in, acc_in, m_ref, l_ref, acc_ref,
    *, block_rows, tok_rows, causal
):
    step = pl.program_id(0)
    span_first = scalars[0]
    seq_place = scalars[1]

    @pl.when(step == 0)
    def _():
        m_ref[...] = m_in[...]
        l_ref[...] = l_in[...]
        acc_ref[...] = acc_in[...]

    if causal:
        group = block_rows // tok_rows
        live = step * group <= seq_place
    else:
        key_first = step * block_rows
        live = key_first < span_first

    @pl.when(live)
    def _():
        q = q_ref[...]
        k = kv_ref[:, :HD]
        v = kv_ref[:, HD:]
        scores = lax.dot_general(
            q, k, (((1,), (1,)), ((), ())), preferred_element_type=jnp.float32
        ) * HD ** (-0.5)
        col = lax.broadcasted_iota(jnp.int32, scores.shape, 1)
        if causal:
            shift = tok_rows.bit_length() - 1
            distance = lax.shift_right_logical(col, shift) + step * group
            row = lax.broadcasted_iota(jnp.int32, scores.shape, 0) & (tok_rows - 1)
            visible = (distance <= seq_place) & (
                (distance > 0) | ((col & (tok_rows - 1)) <= row)
            )
        else:
            visible = col + key_first < span_first
        row_max = m_ref[...]
        new_max = jnp.maximum(row_max, jnp.max(jnp.where(visible, scores, neg_fill), 1, keepdims=True))
        weights = jnp.exp(jnp.where(visible, scores, neg_fill) - new_max)
        rescale = jnp.exp(row_max - new_max)
        l_ref[...] = l_ref[...] * rescale + jnp.sum(weights, 1, keepdims=True)
        acc_ref[...] = acc_ref[...] * rescale + jnp.dot(
            weights.astype(jnp.bfloat16), v, preferred_element_type=jnp.float32
        )
        m_ref[...] = new_max


def flash_pass(scalars, queries, kv_rows, state, block_rows, tok_rows, causal):
    rows = queries.shape[0]
    block_count = kv_rows.shape[0] // block_rows
    if causal:
        def kv_map(j, s):
            return (jnp.minimum(j, s[1] // (block_rows // tok_rows)), 0)
    else:
        def kv_map(j, s):
            last = (s[0] + block_rows - 1) // block_rows - 1
            return (jnp.maximum(jnp.minimum(j, last), 0), 0)
    full = lambda j, s: (0, 0)
    kernel = functools.partial(
        flash_kernel, block_rows=block_rows, tok_rows=tok_rows, causal=causal
    )
    return pl.pallas_call(
        kernel,
        out_shape=(
            jax.ShapeDtypeStruct((rows, 1), jnp.float32),
            jax.ShapeDtypeStruct((rows, 1), jnp.float32),
            jax.ShapeDtypeStruct((rows, HD), jnp.float32),
        ),
        grid_spec=pltpu.PrefetchScalarGridSpec(
            num_scalar_prefetch=1,
            grid=(block_count,),
            in_specs=[
                pl.BlockSpec((rows, HD), full),
                pl.BlockSpec((block_rows, 2 * HD), kv_map),
                pl.BlockSpec((rows, 1), full),
                pl.BlockSpec((rows, 1), full),
                pl.BlockSpec((rows, HD), full),
            ],
            out_specs=[
                pl.BlockSpec((rows, 1), full),
                pl.BlockSpec((rows, 1), full),
                pl.BlockSpec((rows, HD), full),
            ],
        ),
        compiler_params=pltpu.CompilerParams(
            dimension_semantics=("arbitrary",), vmem_limit_bytes=48 * 1024 * 1024
        ),
        cost_estimate=pl.CostEstimate(
            flops=4 * rows * HD * kv_rows.shape[0],
            transcendentals=rows * kv_rows.shape[0],
            bytes_accessed=kv_rows.size * 2 + rows * HD * 6,
        ),
    )(scalars, queries, kv_rows, *state)


def move_pages(finished_cache, block_dest, seq_count, seq_place, kv_width):
    block_total = block_dest.shape[0]
    capacity = 2 * block_total // seq_count
    destination = (block_dest[:, 0] - seq_place) % seq_count
    onehot = (destination[:, None] == jnp.arange(seq_count, dtype=jnp.int32)[None, :]).astype(
        jnp.int32
    )
    earlier_count = jnp.sum((jnp.cumsum(onehot, axis=0, dtype=jnp.int32) - onehot) * onehot, axis=1)
    slot_index = destination * capacity + earlier_count
    slot_match = slot_index[None, :] == jnp.arange(seq_count * capacity, dtype=jnp.int32)[:, None]
    filled = jnp.any(slot_match, axis=1)
    source_block = jnp.sum(
        jnp.where(slot_match, jnp.arange(block_total, dtype=jnp.int32)[None, :], 0), axis=1
    )
    blocks = finished_cache.reshape(LAYERS, block_total, BLK, 2, kv_width)
    outgoing = jnp.where(
        filled[None, :, None, None, None],
        jnp.take(blocks, source_block, axis=1),
        jnp.zeros((), blocks.dtype),
    )
    outgoing = outgoing.reshape(LAYERS, seq_count, capacity * BLK, 2, kv_width)
    piece_rows = capacity * BLK
    page_pool = jnp.zeros((LAYERS, seq_count * piece_rows, 2, kv_width), blocks.dtype)
    for shift in range(seq_count):
        piece = outgoing[:, shift]
        if shift:
            piece = lax.ppermute(
                piece, "seq", [(s, (s + shift) % seq_count) for s in range(seq_count)]
            )
        source = (seq_place - shift) % seq_count
        page_pool = lax.dynamic_update_slice(page_pool, piece, (0, source * piece_rows, 0, 0))
    return page_pool


def on_device(
    tokens,
    norm_gain,
    q_weight,
    kv_weight,
    out_weight,
    ctx_cache,
    span_start,
    finished_cache,
    block_dest,
):
    seq_count = lax.axis_size("seq")
    seq_place = lax.axis_index("seq")
    tok_rows = tokens.shape[0]
    kv_heads = kv_weight.shape[2] // HD
    head_group = q_weight.shape[1] // HD // kv_heads
    kv_width = kv_heads * HD
    ctx_rows = ctx_cache.reshape(ctx_cache.shape[0], 2 * kv_width)
    ctx_all = lax.all_gather(ctx_rows, "seq", axis=0, tiled=True)
    page_pool = move_pages(finished_cache, block_dest, seq_count, seq_place, kv_width)
    gathered = lax.all_gather(tokens, "tp", axis=1, tiled=True)
    widened = gathered.astype(jnp.float32)
    normed = (
        widened
        * lax.rsqrt(jnp.mean(widened * widened, axis=-1, keepdims=True) + rms_eps)
        * norm_gain
    ).astype(jnp.bfloat16)
    span_first = span_start[0]
    positions = (span_first + seq_place * tok_rows + jnp.arange(tok_rows, dtype=jnp.int32)).astype(
        jnp.float32
    )
    queries = jnp.dot(normed, q_weight, preferred_element_type=jnp.float32).reshape(
        tok_rows, kv_heads * head_group, HD
    )
    queries = rotate_pairs(queries, positions).astype(jnp.bfloat16)
    queries = jnp.transpose(queries, (1, 0, 2)).reshape(head_group * tok_rows, HD)
    projected = jnp.dot(
        normed, kv_weight.reshape(D, 2 * kv_width), preferred_element_type=jnp.float32
    ).reshape(tok_rows, 2, kv_heads, HD)
    new_keys = (
        rotate_pairs(projected[:, 0], positions).astype(jnp.bfloat16).reshape(tok_rows, kv_width)
    )
    new_values = projected[:, 1].astype(jnp.bfloat16).reshape(tok_rows, kv_width)
    new_rows = jnp.concatenate([new_keys, new_values], 1)
    arrived = [new_rows]
    for shift in range(1, seq_count):
        arrived.append(
            lax.ppermute(new_rows, "seq", [(s, s + shift) for s in range(seq_count - shift)])
        )
    new_all = jnp.concatenate(arrived, 0)
    query_rows = head_group * tok_rows
    scalars = jnp.stack([span_first, seq_place]).astype(jnp.int32)
    empty_state = (
        jnp.full((query_rows, 1), neg_fill, jnp.float32),
        jnp.zeros((query_rows, 1), jnp.float32),
        jnp.zeros((query_rows, HD), jnp.float32),
    )
    state = flash_pass(scalars, queries, ctx_all, empty_state, CTX_BLOCK, tok_rows, False)
    page_pool, state = lax.optimization_barrier((page_pool, state))
    row_max, row_total, summed = flash_pass(scalars, queries, new_all, state, NEW_BLOCK, tok_rows, True)
    mixed_heads = (
        (summed / row_total)
        .astype(jnp.bfloat16)
        .reshape(head_group, tok_rows, HD)
    )
    mixed_heads = jnp.transpose(mixed_heads, (1, 0, 2)).reshape(tok_rows, kv_width * head_group)
    tp_count = lax.axis_size("tp")
    tp_place = lax.axis_index("tp")
    out_cols = out_weight.shape[1] // tp_count
    partial = jnp.dot(mixed_heads, out_weight, preferred_element_type=jnp.float32)
    reduced = lax.dynamic_slice_in_dim(partial, tp_place * out_cols, out_cols, 1)
    partial = partial.astype(jnp.bfloat16)
    for shift in range(1, tp_count):
        chunk = lax.dynamic_slice_in_dim(
            partial, ((tp_place + shift) % tp_count) * out_cols, out_cols, 1
        )
        reduced = reduced + lax.ppermute(
            chunk, "tp", [(i, (i + shift) % tp_count) for i in range(tp_count)]
        ).astype(jnp.float32)
    attended = reduced.astype(jnp.bfloat16)
    return (attended, page_pool)


def solution(mesh):
    return jax.shard_map(
        on_device,
        mesh=mesh,
        in_specs=(
            P("seq", "tp"),
            P(),
            P(None, "tp"),
            P(None, None, "tp"),
            P("tp", None),
            P("seq", None, "tp"),
            P(),
            P(None, "seq", None, "tp"),
            P("seq", None),
        ),
        out_specs=(P("seq", "tp"), P(None, "seq", None, "tp")),
        check_vma=False,
    )
```

```python
import math
import functools

import jax
import jax.numpy as jnp
from jax import lax
from jax.experimental import pallas as pl
from jax.experimental.pallas import tpu as pltpu
from jax.sharding import PartitionSpec as P

D = 5120
HD = 128
LAYERS = 4
BLK = 16
CTX_BLOCK = 1024


rms_eps = 1e-06
rope_base = 1000000.0
neg_fill = -1e30


def rotate_pairs(values, positions):
    half_width = values.shape[-1] // 2
    frequency = jnp.exp(
        jnp.arange(half_width, dtype=jnp.float32) * (-2.0 * math.log(rope_base) / values.shape[-1])
    )
    angles = positions[:, None] * frequency[None, :]
    cosine = jnp.cos(angles)[:, None, :]
    sine_part = jnp.sin(angles)[:, None, :]
    first_half = values[..., :half_width]
    second_half = values[..., half_width:]
    return jnp.concatenate(
        [
            first_half * cosine - second_half * sine_part,
            second_half * cosine + first_half * sine_part,
        ],
        -1,
    )


def flash_kernel(
    scalars, q_ref, kv_ref, m_in, l_in, acc_in, m_ref, l_ref, acc_ref,
    *, block_rows, tok_rows, causal
):
    step = pl.program_id(0)
    span_first = scalars[0]
    seq_place = scalars[1]

    @pl.when(step == 0)
    def _():
        m_ref[...] = m_in[...]
        l_ref[...] = l_in[...]
        acc_ref[...] = acc_in[...]

    if causal:
        group = block_rows // tok_rows
        live = step * group <= seq_place
    else:
        key_first = step * block_rows
        live = key_first < span_first

    @pl.when(live)
    def _():
        q = q_ref[...]
        k = kv_ref[:, :HD]
        v = kv_ref[:, HD:]
        scores = lax.dot_general(
            q, k, (((1,), (1,)), ((), ())), preferred_element_type=jnp.float32
        ) * HD ** (-0.5)
        col = lax.broadcasted_iota(jnp.int32, scores.shape, 1)
        if causal:
            shift = tok_rows.bit_length() - 1
            distance = lax.shift_right_logical(col, shift) + step * group
            row = lax.broadcasted_iota(jnp.int32, scores.shape, 0) & (tok_rows - 1)
            visible = (distance <= seq_place) & (
                (distance > 0) | ((col & (tok_rows - 1)) <= row)
            )
        else:
            visible = col + key_first < span_first
        row_max = m_ref[...]
        new_max = jnp.maximum(row_max, jnp.max(jnp.where(visible, scores, neg_fill), 1, keepdims=True))
        weights = jnp.where(visible, jnp.exp(scores - new_max), 0.0)
        rescale = jnp.exp(row_max - new_max)
        lane_sum = weights[:, :HD]
        for part in range(1, block_rows // HD):
            lane_sum = lane_sum + weights[:, part * HD:(part + 1) * HD]
        l_ref[...] = l_ref[...] * rescale + lane_sum
        acc_ref[...] = acc_ref[...] * rescale + jnp.dot(
            weights.astype(jnp.bfloat16), v, preferred_element_type=jnp.float32
        )
        m_ref[...] = new_max


def flash_pass(scalars, queries, kv_rows, state, block_rows, tok_rows, causal):
    rows = queries.shape[0]
    block_count = kv_rows.shape[0] // block_rows
    if causal:
        def kv_map(j, s):
            return (jnp.minimum(j, s[1] // (block_rows // tok_rows)), 0)
    else:
        def kv_map(j, s):
            last = (s[0] + block_rows - 1) // block_rows - 1
            return (jnp.maximum(jnp.minimum(j, last), 0), 0)
    full = lambda j, s: (0, 0)
    kernel = functools.partial(
        flash_kernel, block_rows=block_rows, tok_rows=tok_rows, causal=causal
    )
    return pl.pallas_call(
        kernel,
        out_shape=(
            jax.ShapeDtypeStruct((rows, 1), jnp.float32),
            jax.ShapeDtypeStruct((rows, HD), jnp.float32),
            jax.ShapeDtypeStruct((rows, HD), jnp.float32),
        ),
        grid_spec=pltpu.PrefetchScalarGridSpec(
            num_scalar_prefetch=1,
            grid=(block_count,),
            in_specs=[
                pl.BlockSpec((rows, HD), full),
                pl.BlockSpec((block_rows, 2 * HD), kv_map),
                pl.BlockSpec((rows, 1), full),
                pl.BlockSpec((rows, HD), full),
                pl.BlockSpec((rows, HD), full),
            ],
            out_specs=[
                pl.BlockSpec((rows, 1), full),
                pl.BlockSpec((rows, HD), full),
                pl.BlockSpec((rows, HD), full),
            ],
        ),
        compiler_params=pltpu.CompilerParams(
            dimension_semantics=("arbitrary",), vmem_limit_bytes=48 * 1024 * 1024
        ),
        cost_estimate=pl.CostEstimate(
            flops=4 * rows * HD * kv_rows.shape[0],
            transcendentals=rows * kv_rows.shape[0],
            bytes_accessed=kv_rows.size * 2 + rows * HD * 6,
        ),
    )(scalars, queries, kv_rows, *state)


def move_pages(finished_cache, block_dest, seq_count, seq_place, kv_width):
    block_total = block_dest.shape[0]
    capacity = 2 * block_total // seq_count
    destination = (block_dest[:, 0] - seq_place) % seq_count
    onehot = (destination[:, None] == jnp.arange(seq_count, dtype=jnp.int32)[None, :]).astype(
        jnp.int32
    )
    earlier_count = jnp.sum((jnp.cumsum(onehot, axis=0, dtype=jnp.int32) - onehot) * onehot, axis=1)
    slot_index = destination * capacity + earlier_count
    slot_match = slot_index[None, :] == jnp.arange(seq_count * capacity, dtype=jnp.int32)[:, None]
    filled = jnp.any(slot_match, axis=1)
    source_block = jnp.sum(
        jnp.where(slot_match, jnp.arange(block_total, dtype=jnp.int32)[None, :], 0), axis=1
    )
    blocks = finished_cache.reshape(LAYERS, block_total, BLK, 2, kv_width)
    outgoing = jnp.where(
        filled[None, :, None, None, None],
        jnp.take(blocks, source_block, axis=1),
        jnp.zeros((), blocks.dtype),
    )
    outgoing = outgoing.reshape(LAYERS, seq_count, capacity * BLK, 2, kv_width)
    piece_rows = capacity * BLK
    page_pool = jnp.zeros((LAYERS, seq_count * piece_rows, 2, kv_width), blocks.dtype)
    for shift in range(seq_count):
        piece = outgoing[:, shift]
        if shift:
            piece = lax.ppermute(
                piece, "seq", [(s, (s + shift) % seq_count) for s in range(seq_count)]
            )
        source = (seq_place - shift) % seq_count
        page_pool = lax.dynamic_update_slice(page_pool, piece, (0, source * piece_rows, 0, 0))
    return page_pool


def on_device(
    tokens,
    norm_gain,
    q_weight,
    kv_weight,
    out_weight,
    ctx_cache,
    span_start,
    finished_cache,
    block_dest,
):
    seq_count = lax.axis_size("seq")
    seq_place = lax.axis_index("seq")
    tok_rows = tokens.shape[0]
    kv_heads = kv_weight.shape[2] // HD
    head_group = q_weight.shape[1] // HD // kv_heads
    kv_width = kv_heads * HD
    ctx_rows = ctx_cache.reshape(ctx_cache.shape[0], 2 * kv_width)
    ctx_all = lax.all_gather(ctx_rows, "seq", axis=0, tiled=True)
    page_pool = move_pages(finished_cache, block_dest, seq_count, seq_place, kv_width)
    gathered = lax.all_gather(tokens, "tp", axis=1, tiled=True)
    widened = gathered.astype(jnp.float32)
    normed = (
        widened
        * lax.rsqrt(jnp.mean(widened * widened, axis=-1, keepdims=True) + rms_eps)
        * norm_gain
    ).astype(jnp.bfloat16)
    span_first = span_start[0]
    positions = (span_first + seq_place * tok_rows + jnp.arange(tok_rows, dtype=jnp.int32)).astype(
        jnp.float32
    )
    queries = jnp.dot(normed, q_weight, preferred_element_type=jnp.float32).reshape(
        tok_rows, kv_heads * head_group, HD
    )
    queries = rotate_pairs(queries, positions).astype(jnp.bfloat16)
    queries = jnp.transpose(queries, (1, 0, 2)).reshape(head_group * tok_rows, HD)
    projected = jnp.dot(
        normed, kv_weight.reshape(D, 2 * kv_width), preferred_element_type=jnp.float32
    ).reshape(tok_rows, 2, kv_heads, HD)
    new_keys = (
        rotate_pairs(projected[:, 0], positions).astype(jnp.bfloat16).reshape(tok_rows, kv_width)
    )
    new_values = projected[:, 1].astype(jnp.bfloat16).reshape(tok_rows, kv_width)
    new_rows = jnp.concatenate([new_keys, new_values], 1)
    arrived = [new_rows]
    for shift in range(1, seq_count):
        arrived.append(
            lax.ppermute(new_rows, "seq", [(s, s + shift) for s in range(seq_count - shift)])
        )
    new_all = jnp.concatenate(arrived, 0)
    query_rows = head_group * tok_rows
    scalars = jnp.stack([span_first, seq_place]).astype(jnp.int32)
    empty_state = (
        jnp.full((query_rows, 1), neg_fill, jnp.float32),
        jnp.zeros((query_rows, HD), jnp.float32),
        jnp.zeros((query_rows, HD), jnp.float32),
    )
    state = flash_pass(scalars, queries, ctx_all, empty_state, CTX_BLOCK, tok_rows, False)
    page_pool, state = lax.optimization_barrier((page_pool, state))
    row_max, row_total, summed = flash_pass(scalars, queries, new_all, state, CTX_BLOCK, tok_rows, True)
    mixed_heads = (
        (summed / jnp.sum(row_total, 1, keepdims=True))
        .astype(jnp.bfloat16)
        .reshape(head_group, tok_rows, HD)
    )
    mixed_heads = jnp.transpose(mixed_heads, (1, 0, 2)).reshape(tok_rows, kv_width * head_group)
    tp_count = lax.axis_size("tp")
    tp_place = lax.axis_index("tp")
    out_cols = out_weight.shape[1] // tp_count
    partial = jnp.dot(mixed_heads, out_weight, preferred_element_type=jnp.float32)
    reduced = lax.dynamic_slice_in_dim(partial, tp_place * out_cols, out_cols, 1)
    partial = partial.astype(jnp.bfloat16)
    for shift in range(1, tp_count):
        chunk = lax.dynamic_slice_in_dim(
            partial, ((tp_place + shift) % tp_count) * out_cols, out_cols, 1
        )
        reduced = reduced + lax.ppermute(
            chunk, "tp", [(i, (i + shift) % tp_count) for i in range(tp_count)]
        ).astype(jnp.float32)
    attended = reduced.astype(jnp.bfloat16)
    return (attended, page_pool)


def solution(mesh):
    return jax.shard_map(
        on_device,
        mesh=mesh,
        in_specs=(
            P("seq", "tp"),
            P(),
            P(None, "tp"),
            P(None, None, "tp"),
            P("tp", None),
            P("seq", None, "tp"),
            P(),
            P(None, "seq", None, "tp"),
            P("seq", None),
        ),
        out_specs=(P("seq", "tp"), P(None, "seq", None, "tp")),
        check_vma=False,
    )
```
